128 devices in a mesh: wave: 4 (over z), tile: 32 (over x, y, core).
Axes of the slice: x: 4, y: 4, z: 4, core: 2. Of those that a mesh axis runs over, the one named last changes fastest.
Arguments:
- hit_energy: bfloat16 [4096, 32, 128], P('tile', 'wave'), may hold values from -24 to 24
- hit_spot: int32 [4, 4096, 128], P('wave', 'tile'), may hold values from 0 to 511
- block_tile: int32 [4, 4096, 1], P('wave', 'tile'), may hold values from 0 to 31; in each aligned block of 128 rows (0 to 127, 128 to 255, ..., all dimensions but the last counted through in order) at most 8 rows name the same one
- block_count: int32 [4, 4096], P('wave', 'tile'), may hold values from 64 to 128
- block_scene: int32 [4, 4096], P('wave', 'tile'), may hold values from 0 to 3
- block_row: int32 [4, 4096], P('wave', 'tile'), may hold values from 0 to 12
- psf_bank: float32 [64, 32, 961], P(None, 'wave'), may hold values from 0 to 0.004162331
- psf_index: int32 [32, 4, 1], P('tile'), may hold values from 0 to 63
- response: float32 [32, 3], replicated, may hold values from -1 to 1
- conv_in: bfloat16 [64, 3, 3, 3], replicated, may hold values from -1.25 to 1.25
- conv_out: bfloat16 [64, 64, 3, 3], replicated, may hold values from -0.25 to 0.25
Outputs:
- features: bfloat16 [4, 64, 512, 128], P('wave', None, 'tile')
The draws below stay inside these ranges and needn't reach their ends.
Inputs may be any that keep to these rules, and one draw needn't show every extreme that they name: `block_tile`: among the 128 blocks of one device at most 8 name the same tile, a bound that some device reaches.
All inputs are finite; a program needn't handle non-finite values.
Results may differ from the reference program's by a relative error of at most 0.0058.
Values may be sent and summed in bfloat16 or wider, within the bound.
No kernel may reach another device: no remote copies, remote signals or barrier semaphores. Data moves between devices by JAX's collectives and lax.ppermute only.
A program may use at most 64 MiB of HBM per device.

```python
import math
import jax
import jax.numpy as jnp
import numpy as np
from jax import lax

BAND_DEV = 8
BANDS = 32
HITS = 128
NB = 128
CAP = 8
BLOCKS = 4096
ROWS_DEV = 16
W = 128
H = 512
SCENES = 4
WIN = 4
K = 31
PW = 128
PATCHES = 1
NPSF = 64
CH = 64
N_WAVE = 4
N_TILE = 32


def touch_ends(result, rng, smallest, largest):
    shape = result.shape
    index_at = [jax.random.randint(jax.random.fold_in(rng, axis), (), 0, shape[axis]) for axis in range(len(shape))]
    result = result.at[tuple(index_at)].set(smallest)
    longest = shape.index(max(shape))
    index_at[longest] = (index_at[longest] + 1) % shape[longest]
    return result.at[tuple(index_at)].set(largest)


def block_scale(key, dims, cuts, least, largest):
    loudness = 1.0
    for axis_at, parts in cuts:
        heights = jax.random.uniform(jax.random.fold_in(jax.random.fold_in(key, 6), axis_at), (parts,), jnp.float32, least / len(cuts), largest / len(cuts))
        loudness = loudness * jnp.repeat(jnp.exp(heights), dims[axis_at] // parts).reshape((-1,) + (1,) * (len(dims) - 1 - axis_at))
    return loudness


def deal_out(key, own, number, rows, amount, top, bound, lean):
    order = jax.random.permutation(key, amount)
    crowded, usual = shares(amount, rows * top, bound, lean, True), shares(amount, rows * top, bound, lean, False)
    places = jnp.arange(amount)

    def named(lengths, turn):
        used = int((lengths > 0).sum())
        fixed = max(1, used // 4)
        passed = fixed + (places - fixed + turn * (used - fixed)) % max(1, amount - fixed)
        return jnp.zeros((amount,), jnp.int32).at[order[jnp.where(places < fixed, places, passed)]].set(jnp.asarray(lengths, jnp.int32))

    lengths = jnp.where(number % 4 == 0, named(crowded, number // 4), named(usual, number - number // 4 - 1))
    mixed = jax.random.permutation(jax.random.fold_in(own, 3), amount)
    giver, taker = mixed[0:amount // 2 * 2:2], mixed[1:amount // 2 * 2:2]
    slack = jnp.minimum(lengths[giver] - 1, bound - lengths[taker]) // 2
    slack = jnp.where((giver == order[0]) | (taker == order[0]) | (lengths[taker] == 0), 0, jnp.maximum(slack, 0))
    passed = jax.random.randint(jax.random.fold_in(own, 4), (amount // 2,), 0, 1 << 20) % (slack + 1)
    lengths = lengths.at[giver].add(-passed).at[taker].add(passed)
    members = jnp.searchsorted(jnp.cumsum(lengths), jnp.arange(rows * top), side="right").astype(jnp.int32)
    grid = members.reshape(top, rows).T
    grid = grid[jax.random.permutation(jax.random.fold_in(own, 1), rows)]
    turn = jax.random.randint(jax.random.fold_in(own, 2), (rows, 1), 0, top)
    return jnp.take_along_axis(grid, (jnp.arange(top)[None, :] + turn) % top, axis=1)


def shares(number_of, total, bound, skew, full):
    weights = [(1 << 20) // math.isqrt(standing ** skew) + 1 for standing in range(1, number_of + 1)]
    largest = bound if full else min(bound, max(-(-total // number_of), total * weights[0] // sum(weights)))
    least = 1 if total - largest >= number_of - 1 else 0
    holding, rest = [largest] + [least] * (number_of - 1), total - largest - least * (number_of - 1)
    while rest > 0:
        movable = [i for i in range(1, number_of) if holding[i] < largest] or [i for i in range(1, number_of) if holding[i] < bound]
        mass, left = sum([weights[i] for i in movable]), rest
        for i in movable:
            addition = min(bound - holding[i], max(1, left * weights[i] // mass), rest)
            holding[i] = holding[i] + addition
            rest = rest - addition
    return np.array(holding)


def gaussian(key, dims, deviation, bound, shards=(), kind=jnp.bfloat16):
    drawn = deviation * jax.random.normal(key, dims, jnp.float32)
    if shards:
        drawn = drawn * block_scale(key, dims, shards, -0.22, 0.18)
    return jnp.clip(drawn, -bound, bound).astype(kind)


def setup_inputs(seed: int = 0) -> dict:
    keys = jax.random.split(jax.random.key(seed), 12)
    hit_energy = gaussian(keys[0], (BLOCKS, BANDS, HITS), 4.0, 24.0, ((0, 32), (1, 4)))
    hit_spot = touch_ends(jax.random.randint(keys[1], (N_WAVE, BLOCKS, HITS), 0, WIN * W), jax.random.fold_in(keys[1], 1), 0, (WIN * W) - 1).astype(jnp.int32)
    block_tile_keys = jax.random.split(jax.random.fold_in(keys[2], 1), N_WAVE * BLOCKS // NB)
    block_tile_turns = jax.random.permutation(jax.random.fold_in(keys[2], 3), N_WAVE * BLOCKS // NB)
    block_tile = jax.vmap(lambda own, number: deal_out(jax.random.fold_in(keys[2], 2), own, number, NB, N_TILE, 1, CAP, 2))(block_tile_keys, block_tile_turns).reshape((N_WAVE, BLOCKS, 1))
    block_count = touch_ends(jax.random.randint(keys[3], (N_WAVE, BLOCKS), 64, 129), jax.random.fold_in(keys[3], 1), 64, 128).astype(jnp.int32)
    block_scene = touch_ends(jax.random.randint(keys[4], (N_WAVE, BLOCKS), 0, SCENES), jax.random.fold_in(keys[4], 1), 0, SCENES - 1).astype(jnp.int32)
    block_row = touch_ends(jax.random.randint(keys[5], (N_WAVE, BLOCKS), 0, ROWS_DEV - WIN + 1), jax.random.fold_in(keys[5], 1), 0, ROWS_DEV - WIN).astype(jnp.int32)
    psf_bank = jnp.clip(0.004162331 * jax.random.uniform(keys[6], (NPSF, BANDS, K * K), jnp.float32) ** block_scale(keys[6], (NPSF, BANDS, K * K), ((1, 4),), -0.2, 0.2), 0.0, 0.004162331)
    psf_index = touch_ends(jax.random.randint(keys[7], (N_TILE, SCENES, PATCHES), 0, NPSF), jax.random.fold_in(keys[7], 1), 0, NPSF - 1).astype(jnp.int32)
    response = gaussian(keys[8], (BANDS, 3), BANDS ** -0.5, 1.0, (), jnp.float32)
    conv_in = gaussian(keys[9], (CH, 3, 3, 3), 27 ** -0.5, 1.25)
    conv_out = gaussian(keys[10], (CH, CH, 3, 3), (9 * CH) ** -0.5, 0.25)
    return {"hit_energy": hit_energy, "hit_spot": hit_spot, "block_tile": block_tile, "block_count": block_count, "block_scene": block_scene, "block_row": block_row, "psf_bank": psf_bank, "psf_index": psf_index, "response": response, "conv_in": conv_in, "conv_out": conv_out}


def convolve(image, weights):
    return lax.conv_general_dilated(image.astype(jnp.float32), weights.astype(jnp.float32), (1, 1), ((1, 1), (1, 1)), dimension_numbers=("NCHW", "OIHW", "NCHW"), precision=lax.Precision.HIGHEST)


def reference(hit_energy, hit_spot, block_tile, block_count, block_scene, block_row, psf_bank, psf_index, response, conv_in, conv_out):
    radius = K // 2
    lanes = jnp.arange(HITS, dtype=jnp.int32)
    groups = []
    for group in range(N_WAVE):
        energy = hit_energy[:, group * BAND_DEV:(group + 1) * BAND_DEV, :]
        live = lanes[None, :] < block_count[group][:, None]
        masked = jnp.where(live[:, None, :], energy, jnp.zeros_like(energy)).astype(jnp.float32)
        row_top = block_tile[group, :, 0] * ROWS_DEV + block_row[group]
        flat = ((block_scene[group] * H + row_top) * W)[:, None] + hit_spot[group]
        image = jnp.zeros((BAND_DEV, SCENES * H * W), jnp.float32)
        image = image.at[:, flat.reshape(-1)].add(jnp.transpose(masked, (1, 0, 2)).reshape(BAND_DEV, -1))
        groups.append(image.reshape(BAND_DEV, SCENES, H, W))
    splat = jnp.concatenate(groups, axis=0)

    def one_scene(scene):
        plane = lax.dynamic_index_in_dim(splat, scene, 1, keepdims=False)
        padded = jnp.pad(plane, ((0, 0), (radius, radius), (radius, radius)))
        scene_index = lax.dynamic_index_in_dim(psf_index, scene, 1, keepdims=False)

        def one_tile(tile_number):
            strip = lax.dynamic_slice_in_dim(padded, (tile_number * ROWS_DEV).astype(jnp.int32), ROWS_DEV + 2 * radius, 1)
            pieces = jnp.stack([strip[:, :, column * PW:column * PW + PW + 2 * radius] for column in range(PATCHES)], axis=1)
            stacked = pieces.reshape(1, BANDS * PATCHES, ROWS_DEV + 2 * radius, PW + 2 * radius)
            chosen = psf_bank[lax.dynamic_index_in_dim(scene_index, tile_number, 0, keepdims=False)]
            kernels = jnp.transpose(chosen, (1, 0, 2)).reshape(BANDS * PATCHES, 1, K, K)
            out = lax.conv_general_dilated(stacked, kernels, (1, 1), "VALID", dimension_numbers=("NCHW", "OIHW", "NCHW"), feature_group_count=BANDS * PATCHES, precision=lax.Precision.HIGHEST)
            out = out.reshape(BANDS, PATCHES, ROWS_DEV, PW).transpose(0, 2, 1, 3)
            return out.reshape(BANDS, ROWS_DEV, W)

        strips = lax.map(one_tile, jnp.arange(N_TILE, dtype=jnp.int32))
        blurred = jnp.transpose(strips, (1, 0, 2, 3)).reshape(BANDS, H, W)
        color = jnp.einsum("byx,bc->cyx", blurred, response, precision=lax.Precision.HIGHEST)
        sensor = color.astype(jnp.bfloat16)
        hidden = jax.nn.silu(convolve(sensor[None], conv_in)).astype(jnp.bfloat16)
        return convolve(hidden, conv_out)[0].astype(jnp.bfloat16)

    return lax.map(one_scene, jnp.arange(SCENES, dtype=jnp.int32))
```

```python
import math

import jax
import numpy as np
import jax.numpy as jnp
from jax import lax
from jax.sharding import PartitionSpec as P

ROWS_DEV = 16
W = 128
WIN = 4
K = 31


def padded_2(cells, sides, width):
    for axis, dim in sides:
        count = lax.axis_size(axis)
        ends = count - 1
        head = lax.slice_in_dim(cells, 0, width, axis=dim)
        tail = lax.slice_in_dim(cells, cells.shape[dim] - width, cells.shape[dim], axis=dim)
        cells = jnp.concatenate(
            [
                lax.ppermute(tail, axis, [(i, (i + 1) % count) for i in range(ends)]),
                cells,
                lax.ppermute(head, axis, [((i + 1) % count, i) for i in range(ends)]),
            ],
            axis=dim,
        )
    return cells


def conv_rows(image, weights):
    return lax.conv_general_dilated(
        image,
        weights,
        (1, 1),
        ((0, 0), (1, 1)),
        dimension_numbers=("NCHW", "OIHW", "NCHW"),
        preferred_element_type=jnp.float32,
    )


DFT_N = 144


def dft_tables(width, side, radius):
    freqs = DFT_N // 2 + 1
    f = np.arange(freqs)[None, :]
    x = np.arange(width)[:, None]
    angle = 2 * np.pi * f * x / DFT_N
    forward = np.stack([np.cos(angle), -np.sin(angle)]).astype(np.float32)
    lag = (np.arange(side) - radius)[:, None]
    tap_angle = 2 * np.pi * f * lag / DFT_N
    taps = np.stack([np.cos(tap_angle), np.sin(tap_angle)]).astype(np.float32)
    weight = np.full((freqs,), 2.0)
    weight[0] = 1.0
    weight[-1] = 1.0
    back_angle = 2 * np.pi * np.arange(freqs)[:, None] * np.arange(width)[None, :] / DFT_N
    inverse = np.stack(
        [weight[:, None] * np.cos(back_angle), -weight[:, None] * np.sin(back_angle)]
    ) / DFT_N
    return forward, taps, inverse.astype(np.float32)


def patch_blur(extended, psf_bank, psf_index, response, radius):
    band_dev, scenes, tall, width = extended.shape
    rows_dev = tall - 2 * radius
    side = 2 * radius + 1
    forward, taps, inverse = dft_tables(width, side, radius)
    hi = lax.Precision.HIGHEST
    chosen = psf_bank[psf_index[0, :, 0]].reshape(scenes, band_dev, side, side)
    spec_re = jnp.einsum("syx,xf->syf", extended.reshape(band_dev * scenes, tall, width), forward[0], precision=hi)
    spec_im = jnp.einsum("syx,xf->syf", extended.reshape(band_dev * scenes, tall, width), forward[1], precision=hi)
    spec_re = spec_re.reshape(band_dev, scenes, tall, -1)
    spec_im = spec_im.reshape(band_dev, scenes, tall, -1)
    kern_re = jnp.einsum("sbuv,vf->bsuf", chosen, taps[0], precision=hi)
    kern_im = jnp.einsum("sbuv,vf->bsuf", chosen, taps[1], precision=hi)
    out_re = jnp.zeros(spec_re.shape[:2] + (rows_dev, spec_re.shape[3]), jnp.float32)
    out_im = out_re
    for u in range(side):
        xr = spec_re[:, :, u : u + rows_dev]
        xi = spec_im[:, :, u : u + rows_dev]
        kr = kern_re[:, :, u : u + 1]
        ki = kern_im[:, :, u : u + 1]
        out_re = out_re + (kr * xr - ki * xi)
        out_im = out_im + (kr * xi + ki * xr)
    col_re = jnp.einsum("bsyf,bc->scyf", out_re, response, precision=hi)
    col_im = jnp.einsum("bsyf,bc->scyf", out_im, response, precision=hi)
    return jnp.einsum("scyf,fx->scyx", col_re, inverse[0], precision=hi) + jnp.einsum(
        "scyf,fx->scyx", col_im, inverse[1], precision=hi
    )


def window_splat(energy, spots, bases, scenes):
    slots, band_dev, hit_lanes = energy.shape
    group_size = math.gcd(slots, 128)
    steps_total = slots // group_size
    span = WIN * W
    row_total = scenes * ROWS_DEV
    energy = energy.reshape(steps_total, group_size, band_dev, hit_lanes)
    spots = spots.reshape(steps_total, group_size, hit_lanes)
    bases = bases.reshape(steps_total, group_size)
    positions = jnp.arange(span, dtype=jnp.int32)
    offsets = jnp.arange(WIN, dtype=jnp.int32)
    row_ids = jnp.arange(row_total, dtype=jnp.int32)

    def add_group(total, pieces):
        part_energy, part_spot, part_base = pieces
        onehot = (part_spot[:, :, None] == positions[None, None, :]).astype(part_energy.dtype)
        window = jnp.einsum("ibh,ihp->ibp", part_energy, onehot, preferred_element_type=jnp.float32)
        window = window.reshape(group_size, band_dev, WIN, W)
        placing = (
            part_base[:, None, None] + offsets[None, :, None] == row_ids[None, None, :]
        ).astype(jnp.float32)
        added = jnp.einsum("ibjx,ijr->brx", window, placing, precision=lax.Precision.HIGHEST)
        return (total + added, None)

    start = jnp.zeros((band_dev, row_total, W), jnp.float32)
    total, unused = lax.scan(add_group, start, (energy, spots, bases))
    return total.reshape(band_dev, scenes, ROWS_DEV, W)


def per_device(
    hit_energy,
    hit_spot,
    block_tile,
    block_count,
    block_scene,
    block_row,
    psf_bank,
    psf_index,
    response,
    conv_in,
    conv_out,
):
    tile_count = lax.axis_size("tile")
    block_dev, band_dev, hit_lanes = hit_energy.shape
    capacity = 2 * block_dev // tile_count
    scenes = psf_index.shape[1]
    lanes = lax.broadcasted_iota(jnp.int32, (block_dev, hit_lanes), 1)
    live = lanes < block_count[0][:, None]
    masked = jnp.where(live[:, None, :], hit_energy, jnp.zeros_like(hit_energy))
    base_row = block_scene[0] * ROWS_DEV + block_row[0]
    target = block_tile[0, :, 0]
    owners = (target[:, None] == jnp.arange(tile_count, dtype=jnp.int32)[None, :]).astype(jnp.int32)
    before = jnp.cumsum(owners, axis=0) - owners
    place = target * capacity + jnp.sum(before * owners, axis=1)
    send_energy = (
        jnp.zeros((tile_count * capacity, band_dev, hit_lanes), hit_energy.dtype)
        .at[place]
        .set(masked)
    )
    send_spot = jnp.zeros((tile_count * capacity, hit_lanes), jnp.int32).at[place].set(hit_spot[0])
    send_base = jnp.zeros((tile_count * capacity,), jnp.int32).at[place].set(base_row)
    got_energy, got_spot, got_base = (
        lax.all_to_all(send_energy, "tile", split_axis=0, concat_axis=0, tiled=True),
        lax.all_to_all(send_spot, "tile", split_axis=0, concat_axis=0, tiled=True),
        lax.all_to_all(send_base, "tile", split_axis=0, concat_axis=0, tiled=True),
    )
    splat = window_splat(got_energy, got_spot, got_base, scenes)
    extended = padded_2(splat, (("tile", 2),), K // 2)
    wave_index = lax.axis_index("wave")
    band_dev = hit_energy.shape[1]
    my_response = lax.dynamic_slice_in_dim(response, wave_index * band_dev, band_dev, 0)
    partial = patch_blur(extended, psf_bank, psf_index, my_response, K // 2)
    color = lax.psum_scatter(partial, "wave", scatter_dimension=0, tiled=True)
    sensor = color.astype(jnp.bfloat16)
    rimmed = padded_2(sensor, (("tile", 2),), 1)
    hidden = jax.nn.silu(conv_rows(rimmed, conv_in)).astype(jnp.bfloat16)
    hidden_rimmed = padded_2(hidden, (("tile", 2),), 1)
    return conv_rows(hidden_rimmed, conv_out).astype(jnp.bfloat16)


def solution(mesh):
    in_specs = (
        P("tile", "wave", None),
        P("wave", "tile", None),
        P("wave", "tile", None),
        P("wave", "tile"),
        P("wave", "tile"),
        P("wave", "tile"),
        P(None, "wave", None),
        P("tile", None, None),
        P(),
        P(),
        P(),
    )
    out_specs = P("wave", None, "tile", None)
    return jax.shard_map(
        per_device, mesh=mesh, in_specs=in_specs, out_specs=out_specs, check_vma=False
    )
```

```python
import functools

import jax
import jax.numpy as jnp
import numpy as np
from jax import lax
from jax.experimental import pallas as pl
from jax.sharding import PartitionSpec as P

ROWS_DEV = 16
W = 128
WIN = 4
K = 31
DFT_N = 144
LANE = 128
GROUP = 8


def padded_2(cells, sides, width):
    for axis, dim in sides:
        count = lax.axis_size(axis)
        ends = count - 1
        head = lax.slice_in_dim(cells, 0, width, axis=dim)
        tail = lax.slice_in_dim(cells, cells.shape[dim] - width, cells.shape[dim], axis=dim)
        cells = jnp.concatenate(
            [
                lax.ppermute(tail, axis, [(i, (i + 1) % count) for i in range(ends)]),
                cells,
                lax.ppermute(head, axis, [((i + 1) % count, i) for i in range(ends)]),
            ],
            axis=dim,
        )
    return cells


def conv_rows(image, weights):
    return lax.conv_general_dilated(
        image,
        weights,
        (1, 1),
        ((0, 0), (1, 1)),
        dimension_numbers=("NCHW", "OIHW", "NCHW"),
        preferred_element_type=jnp.float32,
    )


def dft_tables(width, side, radius):
    freqs = DFT_N // 2 + 1
    f = np.arange(freqs)[None, :]
    x = np.arange(width)[:, None]
    angle = 2 * np.pi * f * x / DFT_N
    forward = np.zeros((width, 2 * LANE))
    forward[:, :freqs] = np.cos(angle)
    forward[:, LANE : LANE + freqs] = -np.sin(angle)
    lag = (np.arange(side) - radius)[:, None]
    tap_angle = 2 * np.pi * f * lag / DFT_N
    taps = np.zeros((side, 2 * LANE))
    taps[:, :freqs] = np.cos(tap_angle)
    taps[:, LANE : LANE + freqs] = np.sin(tap_angle)
    weight = np.full((freqs,), 2.0)
    weight[0] = 1.0
    weight[-1] = 1.0
    back_angle = 2 * np.pi * np.arange(freqs)[:, None] * np.arange(width)[None, :] / DFT_N
    inverse = np.zeros((2 * LANE, width))
    inverse[:freqs] = weight[:, None] * np.cos(back_angle) / DFT_N
    inverse[LANE : LANE + freqs] = -weight[:, None] * np.sin(back_angle) / DFT_N
    return (
        forward.astype(np.float32),
        taps.astype(np.float32),
        inverse.astype(np.float32),
    )


def row_taps_kernel(spec_ref, kern_ref, out_ref):
    group = spec_ref.shape[0]
    side = kern_ref.shape[1]
    rows = out_ref.shape[1]

    def one(c, carry):
        acc_re = jnp.zeros((rows, LANE), jnp.float32)
        acc_im = jnp.zeros((rows, LANE), jnp.float32)
        for u in range(side):
            xr = spec_ref[c, pl.ds(u, rows), pl.ds(0, LANE)]
            xi = spec_ref[c, pl.ds(u, rows), pl.ds(LANE, LANE)]
            kr = kern_ref[c, pl.ds(u, 1), pl.ds(0, LANE)]
            ki = kern_ref[c, pl.ds(u, 1), pl.ds(LANE, LANE)]
            acc_re = acc_re + (kr * xr - ki * xi)
            acc_im = acc_im + (kr * xi + ki * xr)
        out_ref[c, :, pl.ds(0, LANE)] = acc_re
        out_ref[c, :, pl.ds(LANE, LANE)] = acc_im
        return carry

    lax.fori_loop(0, group, one, 0)


def row_taps(spec, kern, rows):
    channels, tall, both = spec.shape
    side = kern.shape[1]
    return pl.pallas_call(
        row_taps_kernel,
        out_shape=jax.ShapeDtypeStruct((channels, rows, both), jnp.float32),
        grid=(channels // GROUP,),
        in_specs=[
            pl.BlockSpec((GROUP, tall, both), lambda g: (g, 0, 0)),
            pl.BlockSpec((GROUP, side, both), lambda g: (g, 0, 0)),
        ],
        out_specs=pl.BlockSpec((GROUP, rows, both), lambda g: (g, 0, 0)),
    )(spec, kern)


def patch_blur(extended, psf_bank, psf_index, response, radius):
    band_dev, scenes, tall, width = extended.shape
    rows_dev = tall - 2 * radius
    side = 2 * radius + 1
    forward, taps, inverse = dft_tables(width, side, radius)
    hi = lax.Precision.HIGHEST
    chosen = psf_bank[psf_index[0, :, 0]].reshape(scenes, band_dev, side, side)
    chosen = chosen.transpose(1, 0, 2, 3).reshape(band_dev * scenes, side, side)
    spec = jnp.einsum(
        "cyx,xf->cyf", extended.reshape(band_dev * scenes, tall, width), forward, precision=hi
    )
    kern = jnp.einsum("cuv,vf->cuf", chosen, taps, precision=hi)
    out = row_taps(spec, kern, rows_dev).reshape(band_dev, scenes, rows_dev, -1)
    color = jnp.einsum("bsyf,bc->scyf", out, response, precision=hi)
    return jnp.einsum("scyf,fx->scyx", color, inverse, precision=hi)


def window_splat(got, scenes):
    band_dev = got.shape[1] - 2
    energy = got[:, :band_dev]
    field = got[:, band_dev].astype(jnp.int32)
    column = got[:, band_dev + 1].astype(jnp.int32)
    offset = field % WIN
    base = field[:, 0] // WIN
    rows = jnp.arange(WIN, dtype=jnp.int32)
    spread = jnp.where(
        offset[:, None, None, :] == rows[None, None, :, None],
        energy[:, :, None, :],
        jnp.zeros((), energy.dtype),
    )
    onehot = (column[:, :, None] == jnp.arange(W, dtype=jnp.int32)[None, None, :]).astype(
        energy.dtype
    )
    window = jnp.einsum("ibjh,ihc->ibjc", spread, onehot, preferred_element_type=jnp.float32)
    row_ids = jnp.arange(scenes * ROWS_DEV, dtype=jnp.int32)
    placing = (base[:, None, None] + rows[None, :, None] == row_ids[None, None, :]).astype(
        jnp.float32
    )
    total = jnp.einsum("ibjc,ijr->brc", window, placing, precision=lax.Precision.HIGHEST)
    return total.reshape(band_dev, scenes, ROWS_DEV, W)


def per_device(
    hit_energy,
    hit_spot,
    block_tile,
    block_count,
    block_scene,
    block_row,
    psf_bank,
    psf_index,
    response,
    conv_in,
    conv_out,
):
    tile_count = lax.axis_size("tile")
    wave_count = lax.axis_size("wave")
    block_dev, band_dev, hit_lanes = hit_energy.shape
    capacity = 2 * block_dev // tile_count
    scenes = psf_index.shape[1]
    lanes = lax.broadcasted_iota(jnp.int32, (block_dev, hit_lanes), 1)
    live = lanes < block_count[0][:, None]
    masked = jnp.where(live[:, None, :], hit_energy, jnp.zeros_like(hit_energy))
    base_row = block_scene[0] * ROWS_DEV + block_row[0]
    spot = hit_spot[0]
    field = base_row[:, None] * WIN + spot // W
    column = spot % W
    payload = jnp.concatenate(
        [
            masked,
            field.astype(hit_energy.dtype)[:, None, :],
            column.astype(hit_energy.dtype)[:, None, :],
        ],
        axis=1,
    )
    target = block_tile[0, :, 0]
    owners = (target[:, None] == jnp.arange(tile_count, dtype=jnp.int32)[None, :]).astype(jnp.int32)
    before = jnp.cumsum(owners, axis=0) - owners
    place = target * capacity + jnp.sum(before * owners, axis=1)
    slots = jnp.arange(tile_count * capacity, dtype=jnp.int32)
    select = (slots[:, None] == place[None, :]).astype(hit_energy.dtype)
    send = jnp.einsum(
        "pi,ibh->pbh", select, payload, preferred_element_type=jnp.float32
    ).astype(hit_energy.dtype)
    got = lax.all_to_all(send, "tile", split_axis=0, concat_axis=0, tiled=True)
    splat = window_splat(got, scenes)
    extended = padded_2(splat, (("tile", 2),), K // 2)
    wave_index = lax.axis_index("wave")
    my_response = lax.dynamic_slice_in_dim(response, wave_index * band_dev, band_dev, 0)
    partial = patch_blur(extended, psf_bank, psf_index, my_response, K // 2)
    color = lax.dynamic_index_in_dim(partial, wave_index, 0, keepdims=False)
    for step in range(1, wave_count):
        piece = lax.dynamic_index_in_dim(partial, (wave_index + step) % wave_count, 0, keepdims=False)
        color = color + lax.ppermute(
            piece, "wave", [(i, (i + step) % wave_count) for i in range(wave_count)]
        )
    sensor = color[None].astype(jnp.bfloat16)
    rimmed = padded_2(sensor, (("tile", 2),), 1)
    hidden = jax.nn.silu(conv_rows(rimmed, conv_in)).astype(jnp.bfloat16)
    hidden_rimmed = padded_2(hidden, (("tile", 2),), 1)
    return conv_rows(hidden_rimmed, conv_out).astype(jnp.bfloat16)


def solution(mesh):
    in_specs = (
        P("tile", "wave", None),
        P("wave", "tile", None),
        P("wave", "tile", None),
        P("wave", "tile"),
        P("wave", "tile"),
        P("wave", "tile"),
        P(None, "wave", None),
        P("tile", None, None),
        P(),
        P(),
        P(),
    )
    out_specs = P("wave", None, "tile", None)
    return jax.shard_map(
        per_device, mesh=mesh, in_specs=in_specs, out_specs=out_specs, check_vma=False
    )
```

```python
import functools

import jax
import jax.numpy as jnp
import numpy as np
from jax import lax
from jax.experimental import pallas as pl
from jax.sharding import PartitionSpec as P

ROWS_DEV = 16
W = 128
WIN = 4
K = 31
DFT_N = 144
LANE = 128
GROUP = 8


def padded_2(cells, sides, width):
    for axis, dim in sides:
        count = lax.axis_size(axis)
        ends = count - 1
        head = lax.slice_in_dim(cells, 0, width, axis=dim)
        tail = lax.slice_in_dim(cells, cells.shape[dim] - width, cells.shape[dim], axis=dim)
        cells = jnp.concatenate(
            [
                lax.ppermute(tail, axis, [(i, (i + 1) % count) for i in range(ends)]),
                cells,
                lax.ppermute(head, axis, [((i + 1) % count, i) for i in range(ends)]),
            ],
            axis=dim,
        )
    return cells


def conv_rows(image, weights):
    return lax.conv_general_dilated(
        image,
        weights,
        (1, 1),
        ((0, 0), (1, 1)),
        dimension_numbers=("NCHW", "OIHW", "NCHW"),
        preferred_element_type=jnp.float32,
    )


def dft_tables(width, side, radius):
    freqs = DFT_N // 2 + 1
    f = np.arange(freqs)[None, :]
    x = np.arange(width)[:, None]
    angle = 2 * np.pi * f * x / DFT_N
    forward = np.zeros((width, 2 * LANE))
    forward[:, :freqs] = np.cos(angle)
    forward[:, LANE : LANE + freqs] = -np.sin(angle)
    lag = (np.arange(side) - radius)[:, None]
    tap_angle = 2 * np.pi * f * lag / DFT_N
    taps = np.zeros((side, 2 * LANE))
    taps[:, :freqs] = np.cos(tap_angle)
    taps[:, LANE : LANE + freqs] = np.sin(tap_angle)
    weight = np.full((freqs,), 2.0)
    weight[0] = 1.0
    weight[-1] = 1.0
    back_angle = 2 * np.pi * np.arange(freqs)[:, None] * np.arange(width)[None, :] / DFT_N
    inverse = np.zeros((2 * LANE, width))
    inverse[:freqs] = weight[:, None] * np.cos(back_angle) / DFT_N
    inverse[LANE : LANE + freqs] = -weight[:, None] * np.sin(back_angle) / DFT_N
    return (
        forward.astype(np.float32),
        taps.astype(np.float32),
        inverse.astype(np.float32),
    )


def row_taps_kernel(spec_ref, kern_ref, out_ref):
    group = spec_ref.shape[0]
    side = kern_ref.shape[1]
    rows = out_ref.shape[1]

    def one(c, carry):
        acc_re = jnp.zeros((rows, LANE), jnp.float32)
        acc_im = jnp.zeros((rows, LANE), jnp.float32)
        for u in range(side):
            xr = spec_ref[c, pl.ds(u, rows), pl.ds(0, LANE)]
            xi = spec_ref[c, pl.ds(u, rows), pl.ds(LANE, LANE)]
            kr = kern_ref[c, pl.ds(u, 1), pl.ds(0, LANE)]
            ki = kern_ref[c, pl.ds(u, 1), pl.ds(LANE, LANE)]
            acc_re = acc_re + (kr * xr - ki * xi)
            acc_im = acc_im + (kr * xi + ki * xr)
        out_ref[c, :, pl.ds(0, LANE)] = acc_re
        out_ref[c, :, pl.ds(LANE, LANE)] = acc_im
        return carry

    lax.fori_loop(0, group, one, 0)


def row_taps(spec, kern, rows):
    channels, tall, both = spec.shape
    side = kern.shape[1]
    return pl.pallas_call(
        row_taps_kernel,
        out_shape=jax.ShapeDtypeStruct((channels, rows, both), jnp.float32),
        grid=(channels // GROUP,),
        in_specs=[
            pl.BlockSpec((GROUP, tall, both), lambda g: (g, 0, 0)),
            pl.BlockSpec((GROUP, side, both), lambda g: (g, 0, 0)),
        ],
        out_specs=pl.BlockSpec((GROUP, rows, both), lambda g: (g, 0, 0)),
    )(spec, kern)


def patch_blur(extended, psf_bank, psf_index, response, radius):
    band_dev, scenes, tall, width = extended.shape
    rows_dev = tall - 2 * radius
    side = 2 * radius + 1
    forward, taps, inverse = dft_tables(width, side, radius)
    hi = lax.Precision.HIGHEST
    chosen = psf_bank[psf_index[0, :, 0]].reshape(scenes, band_dev, side, side)
    chosen = chosen.transpose(1, 0, 2, 3).reshape(band_dev * scenes, side, side)
    spec = jnp.einsum(
        "cyx,xf->cyf", extended.reshape(band_dev * scenes, tall, width), forward, precision=hi
    )
    kern = jnp.einsum("cuv,vf->cuf", chosen, taps, precision=hi)
    out = row_taps(spec, kern, rows_dev).reshape(band_dev, scenes, rows_dev, -1)
    color = jnp.einsum("bsyf,bc->scyf", out, response, precision=hi)
    return jnp.einsum("scyf,fx->scyx", color, inverse, precision=hi)


def window_splat(got, scenes):
    band_dev = got.shape[1] - 2
    energy = got[:, :band_dev]
    field = got[:, band_dev].astype(jnp.int32)
    column = got[:, band_dev + 1].astype(jnp.int32)
    offset = field % WIN
    base = field[:, 0] // WIN
    rows = jnp.arange(WIN, dtype=jnp.int32)
    spread = jnp.where(
        offset[:, None, None, :] == rows[None, None, :, None],
        energy[:, :, None, :],
        jnp.zeros((), energy.dtype),
    )
    onehot = (column[:, :, None] == jnp.arange(W, dtype=jnp.int32)[None, None, :]).astype(
        energy.dtype
    )
    window = jnp.einsum("ibjh,ihc->ibjc", spread, onehot, preferred_element_type=jnp.float32)
    row_ids = jnp.arange(scenes * ROWS_DEV, dtype=jnp.int32)
    placing = (base[:, None, None] + rows[None, :, None] == row_ids[None, None, :]).astype(
        jnp.float32
    )
    placing = placing.astype(jnp.bfloat16)
    upper = window.astype(jnp.bfloat16)
    lower = (window - upper.astype(jnp.float32)).astype(jnp.bfloat16)
    total = jnp.einsum(
        "ibjc,ijr->brc", upper, placing, preferred_element_type=jnp.float32
    ) + jnp.einsum("ibjc,ijr->brc", lower, placing, preferred_element_type=jnp.float32)
    return total.reshape(band_dev, scenes, ROWS_DEV, W)


def per_device(
    hit_energy,
    hit_spot,
    block_tile,
    block_count,
    block_scene,
    block_row,
    psf_bank,
    psf_index,
    response,
    conv_in,
    conv_out,
):
    tile_count = lax.axis_size("tile")
    wave_count = lax.axis_size("wave")
    block_dev, band_dev, hit_lanes = hit_energy.shape
    capacity = 2 * block_dev // tile_count
    scenes = psf_index.shape[1]
    lanes = lax.broadcasted_iota(jnp.int32, (block_dev, hit_lanes), 1)
    live = lanes < block_count[0][:, None]
    masked = jnp.where(live[:, None, :], hit_energy, jnp.zeros_like(hit_energy))
    base_row = block_scene[0] * ROWS_DEV + block_row[0]
    spot = hit_spot[0]
    field = base_row[:, None] * WIN + spot // W
    column = spot % W
    payload = jnp.concatenate(
        [
            masked,
            field.astype(hit_energy.dtype)[:, None, :],
            column.astype(hit_energy.dtype)[:, None, :],
        ],
        axis=1,
    )
    target = block_tile[0, :, 0]
    owners = (target[:, None] == jnp.arange(tile_count, dtype=jnp.int32)[None, :]).astype(jnp.int32)
    order = lax.broadcasted_iota(jnp.int32, (block_dev, block_dev), 0)
    earlier = (order > order.T).astype(jnp.bfloat16)
    before = jnp.dot(earlier, owners.astype(jnp.bfloat16), preferred_element_type=jnp.float32)
    rank = jnp.sum(before * owners.astype(jnp.float32), axis=1).astype(jnp.int32)
    place = target * capacity + rank
    slots = jnp.arange(tile_count * capacity, dtype=jnp.int32)
    select = (slots[:, None] == place[None, :]).astype(hit_energy.dtype)
    send = jnp.einsum(
        "pi,ibh->pbh", select, payload, preferred_element_type=jnp.float32
    ).astype(hit_energy.dtype)
    got = lax.all_to_all(send, "tile", split_axis=0, concat_axis=0, tiled=True)
    splat = window_splat(got, scenes)
    extended = padded_2(splat, (("tile", 2),), K // 2)
    wave_index = lax.axis_index("wave")
    my_response = lax.dynamic_slice_in_dim(response, wave_index * band_dev, band_dev, 0)
    partial = patch_blur(extended, psf_bank, psf_index, my_response, K // 2)
    color = lax.dynamic_index_in_dim(partial, wave_index, 0, keepdims=False)
    for step in range(1, wave_count):
        piece = lax.dynamic_index_in_dim(partial, (wave_index + step) % wave_count, 0, keepdims=False)
        color = color + lax.ppermute(
            piece, "wave", [(i, (i + step) % wave_count) for i in range(wave_count)]
        )
    sensor = color[None].astype(jnp.bfloat16)
    rimmed = padded_2(sensor, (("tile", 2),), 2)
    hidden = jax.nn.silu(conv_rows(rimmed, conv_in)).astype(jnp.bfloat16)
    tile_index = lax.axis_index("tile")
    row_ids = lax.broadcasted_iota(jnp.int32, hidden.shape, 2)
    outside = ((tile_index == 0) & (row_ids == 0)) | (
        (tile_index == tile_count - 1) & (row_ids == hidden.shape[2] - 1)
    )
    hidden = jnp.where(outside, jnp.zeros_like(hidden), hidden)
    return conv_rows(hidden, conv_out).astype(jnp.bfloat16)


def solution(mesh):
    in_specs = (
        P("tile", "wave", None),
        P("wave", "tile", None),
        P("wave", "tile", None),
        P("wave", "tile"),
        P("wave", "tile"),
        P("wave", "tile"),
        P(None, "wave", None),
        P("tile", None, None),
        P(),
        P(),
        P(),
    )
    out_specs = P("wave", None, "tile", None)
    return jax.shard_map(
        per_device, mesh=mesh, in_specs=in_specs, out_specs=out_specs, check_vma=False
    )
```

```python
import functools

import jax
import jax.numpy as jnp
import numpy as np
from jax import lax
from jax.experimental import pallas as pl
from jax.sharding import PartitionSpec as P

ROWS_DEV = 16
W = 128
WIN = 4
K = 31
DFT_N = 144
LANE = 128
GROUP = 8


def padded_2(cells, sides, width):
    for axis, dim in sides:
        count = lax.axis_size(axis)
        ends = count - 1
        head = lax.slice_in_dim(cells, 0, width, axis=dim)
        tail = lax.slice_in_dim(cells, cells.shape[dim] - width, cells.shape[dim], axis=dim)
        cells = jnp.concatenate(
            [
                lax.ppermute(tail, axis, [(i, (i + 1) % count) for i in range(ends)]),
                cells,
                lax.ppermute(head, axis, [((i + 1) % count, i) for i in range(ends)]),
            ],
            axis=dim,
        )
    return cells


def conv_rows(image, weights):
    return lax.conv_general_dilated(
        image,
        weights,
        (1, 1),
        ((0, 0), (1, 1)),
        dimension_numbers=("NCHW", "OIHW", "NCHW"),
        preferred_element_type=jnp.float32,
    )


def dft_tables(width, side, radius):
    freqs = DFT_N // 2 + 1
    f = np.arange(freqs)[None, :]
    x = np.arange(width)[:, None]
    angle = 2 * np.pi * f * x / DFT_N
    forward = np.zeros((width, 2 * LANE))
    forward[:, :freqs] = np.cos(angle)
    forward[:, LANE : LANE + freqs] = -np.sin(angle)
    lag = (np.arange(side) - radius)[:, None]
    tap_angle = 2 * np.pi * f * lag / DFT_N
    taps = np.zeros((side, 2 * LANE))
    taps[:, :freqs] = np.cos(tap_angle)
    taps[:, LANE : LANE + freqs] = np.sin(tap_angle)
    weight = np.full((freqs,), 2.0)
    weight[0] = 1.0
    weight[-1] = 1.0
    back_angle = 2 * np.pi * np.arange(freqs)[:, None] * np.arange(width)[None, :] / DFT_N
    inverse = np.zeros((2 * LANE, width))
    inverse[:freqs] = weight[:, None] * np.cos(back_angle) / DFT_N
    inverse[LANE : LANE + freqs] = -weight[:, None] * np.sin(back_angle) / DFT_N
    return (
        forward.astype(np.float32),
        taps.astype(np.float32),
        inverse.astype(np.float32),
    )


def row_taps_kernel(spec_ref, kern_ref, out_ref):
    group = spec_ref.shape[0]
    side = kern_ref.shape[1]
    rows = out_ref.shape[1]

    def one(c, carry):
        acc_re = jnp.zeros((rows, LANE), jnp.float32)
        acc_im = jnp.zeros((rows, LANE), jnp.float32)
        for u in range(side):
            xr = spec_ref[c, pl.ds(u, rows), pl.ds(0, LANE)]
            xi = spec_ref[c, pl.ds(u, rows), pl.ds(LANE, LANE)]
            kr = kern_ref[c, pl.ds(u, 1), pl.ds(0, LANE)]
            ki = kern_ref[c, pl.ds(u, 1), pl.ds(LANE, LANE)]
            acc_re = acc_re + (kr * xr - ki * xi)
            acc_im = acc_im + (kr * xi + ki * xr)
        out_ref[c, :, pl.ds(0, LANE)] = acc_re
        out_ref[c, :, pl.ds(LANE, LANE)] = acc_im
        return carry

    lax.fori_loop(0, group, one, 0)


def row_taps(spec, kern, rows):
    channels, tall, both = spec.shape
    side = kern.shape[1]
    return pl.pallas_call(
        row_taps_kernel,
        out_shape=jax.ShapeDtypeStruct((channels, rows, both), jnp.float32),
        grid=(channels // GROUP,),
        in_specs=[
            pl.BlockSpec((GROUP, tall, both), lambda g: (g, 0, 0)),
            pl.BlockSpec((GROUP, side, both), lambda g: (g, 0, 0)),
        ],
        out_specs=pl.BlockSpec((GROUP, rows, both), lambda g: (g, 0, 0)),
    )(spec, kern)


def kernel_spectra(psf_bank, psf_index, radius):
    scenes = psf_index.shape[1]
    band_dev = psf_bank.shape[1]
    side = 2 * radius + 1
    unused, taps, unused_too = dft_tables(W, side, radius)
    chosen = psf_bank[psf_index[0, :, 0]].reshape(scenes, band_dev, side, side)
    return jnp.einsum("sbuv,vf->sbuf", chosen, taps, precision=lax.Precision.HIGHEST)


def scene_blur(extended, kern, response, scene, radius):
    band_dev, scenes, tall, width = extended.shape
    rows_dev = tall - 2 * radius
    side = 2 * radius + 1
    forward, unused, inverse = dft_tables(width, side, radius)
    hi = lax.Precision.HIGHEST
    plane = lax.dynamic_index_in_dim(extended, scene, 1, keepdims=False)
    taps = lax.dynamic_index_in_dim(kern, scene, 0, keepdims=False)
    spec = jnp.einsum("byx,xf->byf", plane, forward, precision=hi)
    out = row_taps(spec, taps, rows_dev)
    color = jnp.einsum("byf,bc->cyf", out, response, precision=hi)
    return jnp.einsum("cyf,fx->cyx", color, inverse, precision=hi)


def window_splat(got, scenes):
    band_dev = got.shape[1] - 2
    energy = got[:, :band_dev]
    field = got[:, band_dev].astype(jnp.int32)
    column = got[:, band_dev + 1].astype(jnp.int32)
    offset = field % WIN
    base = field[:, 0] // WIN
    rows = jnp.arange(WIN, dtype=jnp.int32)
    spread = jnp.where(
        offset[:, None, None, :] == rows[None, None, :, None],
        energy[:, :, None, :],
        jnp.zeros((), energy.dtype),
    )
    onehot = (column[:, :, None] == jnp.arange(W, dtype=jnp.int32)[None, None, :]).astype(
        energy.dtype
    )
    window = jnp.einsum("ibjh,ihc->ibjc", spread, onehot, preferred_element_type=jnp.float32)
    row_ids = jnp.arange(scenes * ROWS_DEV, dtype=jnp.int32)
    placing = (base[:, None, None] + rows[None, :, None] == row_ids[None, None, :]).astype(
        jnp.float32
    )
    total = jnp.einsum("ibjc,ijr->brc", window, placing, precision=lax.Precision.HIGH)
    return total.reshape(band_dev, scenes, ROWS_DEV, W)


def per_device(
    hit_energy,
    hit_spot,
    block_tile,
    block_count,
    block_scene,
    block_row,
    psf_bank,
    psf_index,
    response,
    conv_in,
    conv_out,
):
    tile_count = lax.axis_size("tile")
    wave_count = lax.axis_size("wave")
    block_dev, band_dev, hit_lanes = hit_energy.shape
    capacity = 2 * block_dev // tile_count
    scenes = psf_index.shape[1]
    lanes = lax.broadcasted_iota(jnp.int32, (block_dev, hit_lanes), 1)
    live = lanes < block_count[0][:, None]
    masked = jnp.where(live[:, None, :], hit_energy, jnp.zeros_like(hit_energy))
    base_row = block_scene[0] * ROWS_DEV + block_row[0]
    spot = hit_spot[0]
    field = base_row[:, None] * WIN + spot // W
    column = spot % W
    payload = jnp.concatenate(
        [
            masked,
            field.astype(hit_energy.dtype)[:, None, :],
            column.astype(hit_energy.dtype)[:, None, :],
        ],
        axis=1,
    )
    target = block_tile[0, :, 0]
    owners = (target[:, None] == jnp.arange(tile_count, dtype=jnp.int32)[None, :]).astype(jnp.int32)
    order = lax.broadcasted_iota(jnp.int32, (block_dev, block_dev), 0)
    earlier = (order > order.T).astype(jnp.bfloat16)
    before = jnp.dot(earlier, owners.astype(jnp.bfloat16), preferred_element_type=jnp.float32)
    rank = jnp.sum(before * owners.astype(jnp.float32), axis=1).astype(jnp.int32)
    place = target * capacity + rank
    slots = jnp.arange(tile_count * capacity, dtype=jnp.int32)
    select = (slots[:, None] == place[None, :]).astype(hit_energy.dtype)
    send = jnp.einsum(
        "pi,ibh->pbh", select, payload, preferred_element_type=jnp.float32
    ).astype(hit_energy.dtype)
    kern = kernel_spectra(psf_bank, psf_index, K // 2)
    got = lax.all_to_all(send, "tile", split_axis=0, concat_axis=0, tiled=True)
    splat = window_splat(got, scenes)
    extended = padded_2(splat, (("tile", 2),), K // 2)
    wave_index = lax.axis_index("wave")
    my_response = lax.dynamic_slice_in_dim(response, wave_index * band_dev, band_dev, 0)
    color = None
    for step in list(range(1, wave_count)) + [0]:
        scene = (wave_index + step) % wave_count
        piece = scene_blur(extended, kern, my_response, scene, K // 2)
        if step:
            piece = lax.ppermute(
                piece, "wave", [(i, (i + step) % wave_count) for i in range(wave_count)]
            )
        color = piece if color is None else color + piece
    sensor = lax.reduce_precision(color[None], exponent_bits=8, mantissa_bits=7)
    sensor = sensor.astype(jnp.bfloat16)
    rimmed = padded_2(sensor, (("tile", 2),), 2)
    hidden = jax.nn.silu(conv_rows(rimmed, conv_in))
    hidden = lax.reduce_precision(hidden, exponent_bits=8, mantissa_bits=7).astype(jnp.bfloat16)
    tile_index = lax.axis_index("tile")
    row_ids = lax.broadcasted_iota(jnp.int32, hidden.shape, 2)
    outside = ((tile_index == 0) & (row_ids == 0)) | (
        (tile_index == tile_count - 1) & (row_ids == hidden.shape[2] - 1)
    )
    hidden = jnp.where(outside, jnp.zeros_like(hidden), hidden)
    return conv_rows(hidden, conv_out).astype(jnp.bfloat16)


def solution(mesh):
    in_specs = (
        P("tile", "wave", None),
        P("wave", "tile", None),
        P("wave", "tile", None),
        P("wave", "tile"),
        P("wave", "tile"),
        P("wave", "tile"),
        P(None, "wave", None),
        P("tile", None, None),
        P(),
        P(),
        P(),
    )
    out_specs = P("wave", None, "tile", None)
    return jax.shard_map(
        per_device, mesh=mesh, in_specs=in_specs, out_specs=out_specs, check_vma=False
    )
```

```python
import functools

import jax
import jax.numpy as jnp
import numpy as np
from jax import lax
from jax.experimental import pallas as pl
from jax.sharding import PartitionSpec as P

ROWS_DEV = 16
W = 128
WIN = 4
K = 31
DFT_N = 144
LANE = 128
GROUP = 8


def padded_2(cells, sides, width):
    for axis, dim in sides:
        count = lax.axis_size(axis)
        ends = count - 1
        head = lax.slice_in_dim(cells, 0, width, axis=dim)
        tail = lax.slice_in_dim(cells, cells.shape[dim] - width, cells.shape[dim], axis=dim)
        cells = jnp.concatenate(
            [
                lax.ppermute(tail, axis, [(i, (i + 1) % count) for i in range(ends)]),
                cells,
                lax.ppermute(head, axis, [((i + 1) % count, i) for i in range(ends)]),
            ],
            axis=dim,
        )
    return cells


def conv_rows(image, weights):
    return lax.conv_general_dilated(
        image,
        weights,
        (1, 1),
        ((0, 0), (1, 1)),
        dimension_numbers=("NCHW", "OIHW", "NCHW"),
        preferred_element_type=jnp.float32,
    )


def dft_tables(width, side, radius):
    freqs = DFT_N // 2 + 1
    f = np.arange(freqs)[None, :]
    x = np.arange(width)[:, None]
    angle = 2 * np.pi * f * x / DFT_N
    forward = np.zeros((width, 2 * LANE))
    forward[:, :freqs] = np.cos(angle)
    forward[:, LANE : LANE + freqs] = -np.sin(angle)
    lag = (np.arange(side) - radius)[:, None]
    tap_angle = 2 * np.pi * f * lag / DFT_N
    taps = np.zeros((side, 2 * LANE))
    taps[:, :freqs] = np.cos(tap_angle)
    taps[:, LANE : LANE + freqs] = np.sin(tap_angle)
    weight = np.full((freqs,), 2.0)
    weight[0] = 1.0
    weight[-1] = 1.0
    back_angle = 2 * np.pi * np.arange(freqs)[:, None] * np.arange(width)[None, :] / DFT_N
    inverse = np.zeros((2 * LANE, width))
    inverse[:freqs] = weight[:, None] * np.cos(back_angle) / DFT_N
    inverse[LANE : LANE + freqs] = -weight[:, None] * np.sin(back_angle) / DFT_N
    return (
        forward.astype(np.float32),
        taps.astype(np.float32),
        inverse.astype(np.float32),
    )


def row_taps_kernel(spec_ref, kern_ref, out_ref):
    group = spec_ref.shape[0]
    side = kern_ref.shape[1]
    rows = out_ref.shape[1]

    def one(c, carry):
        acc_re = jnp.zeros((rows, LANE), jnp.float32)
        acc_im = jnp.zeros((rows, LANE), jnp.float32)
        for u in range(side):
            xr = spec_ref[c, pl.ds(u, rows), pl.ds(0, LANE)]
            xi = spec_ref[c, pl.ds(u, rows), pl.ds(LANE, LANE)]
            kr = kern_ref[c, pl.ds(u, 1), pl.ds(0, LANE)]
            ki = kern_ref[c, pl.ds(u, 1), pl.ds(LANE, LANE)]
            acc_re = acc_re + (kr * xr - ki * xi)
            acc_im = acc_im + (kr * xi + ki * xr)
        out_ref[c, :, pl.ds(0, LANE)] = acc_re
        out_ref[c, :, pl.ds(LANE, LANE)] = acc_im
        return carry

    lax.fori_loop(0, group, one, 0)


def row_taps(spec, kern, rows):
    channels, tall, both = spec.shape
    side = kern.shape[1]
    return pl.pallas_call(
        row_taps_kernel,
        out_shape=jax.ShapeDtypeStruct((channels, rows, both), jnp.float32),
        grid=(channels // GROUP,),
        in_specs=[
            pl.BlockSpec((GROUP, tall, both), lambda g: (g, 0, 0)),
            pl.BlockSpec((GROUP, side, both), lambda g: (g, 0, 0)),
        ],
        out_specs=pl.BlockSpec((GROUP, rows, both), lambda g: (g, 0, 0)),
    )(spec, kern)


def kernel_spectra(psf_bank, psf_index, radius):
    scenes = psf_index.shape[1]
    band_dev = psf_bank.shape[1]
    side = 2 * radius + 1
    unused, taps, unused_too = dft_tables(W, side, radius)
    chosen = psf_bank[psf_index[0, :, 0]].reshape(scenes, band_dev, side, side)
    return jnp.einsum("sbuv,vf->sbuf", chosen, taps, precision=lax.Precision.HIGHEST)


def patch_blur(extended, kern, response, radius):
    band_dev, scenes, tall, width = extended.shape
    rows_dev = tall - 2 * radius
    side = 2 * radius + 1
    forward, unused, inverse = dft_tables(width, side, radius)
    hi = lax.Precision.HIGHEST
    spec = jnp.einsum(
        "cyx,xf->cyf", extended.reshape(band_dev * scenes, tall, width), forward, precision=hi
    )
    taps = kern.transpose(1, 0, 2, 3).reshape(band_dev * scenes, side, -1)
    out = row_taps(spec, taps, rows_dev).reshape(band_dev, scenes, rows_dev, -1)
    color = jnp.einsum("bsyf,bc->scyf", out, response, precision=hi)
    return jnp.einsum("scyf,fx->scyx", color, inverse, precision=hi)


def window_splat(got, scenes):
    band_dev = got.shape[1] - 2
    energy = got[:, :band_dev]
    field = got[:, band_dev].astype(jnp.int32)
    column = got[:, band_dev + 1].astype(jnp.int32)
    offset = field % WIN
    base = field[:, 0] // WIN
    rows = jnp.arange(WIN, dtype=jnp.int32)
    spread = jnp.where(
        offset[:, None, None, :] == rows[None, None, :, None],
        energy[:, :, None, :],
        jnp.zeros((), energy.dtype),
    )
    onehot = (column[:, :, None] == jnp.arange(W, dtype=jnp.int32)[None, None, :]).astype(
        energy.dtype
    )
    window = jnp.einsum("ibjh,ihc->ibjc", spread, onehot, preferred_element_type=jnp.float32)
    row_ids = jnp.arange(scenes * ROWS_DEV, dtype=jnp.int32)
    placing = (base[:, None, None] + rows[None, :, None] == row_ids[None, None, :]).astype(
        jnp.float32
    )
    total = jnp.einsum("ibjc,ijr->brc", window, placing, precision=lax.Precision.HIGH)
    return total.reshape(band_dev, scenes, ROWS_DEV, W)


def per_device(
    hit_energy,
    hit_spot,
    block_tile,
    block_count,
    block_scene,
    block_row,
    psf_bank,
    psf_index,
    response,
    conv_in,
    conv_out,
):
    tile_count = lax.axis_size("tile")
    wave_count = lax.axis_size("wave")
    block_dev, band_dev, hit_lanes = hit_energy.shape
    capacity = 2 * block_dev // tile_count
    scenes = psf_index.shape[1]
    lanes = lax.broadcasted_iota(jnp.int32, (block_dev, hit_lanes), 1)
    live = lanes < block_count[0][:, None]
    masked = jnp.where(live[:, None, :], hit_energy, jnp.zeros_like(hit_energy))
    base_row = block_scene[0] * ROWS_DEV + block_row[0]
    spot = hit_spot[0]
    field = base_row[:, None] * WIN + spot // W
    column = spot % W
    payload = jnp.concatenate(
        [
            masked,
            field.astype(hit_energy.dtype)[:, None, :],
            column.astype(hit_energy.dtype)[:, None, :],
        ],
        axis=1,
    )
    target = block_tile[0, :, 0]
    owners = (target[:, None] == jnp.arange(tile_count, dtype=jnp.int32)[None, :]).astype(jnp.int32)
    order = lax.broadcasted_iota(jnp.int32, (block_dev, block_dev), 0)
    earlier = (order > order.T).astype(jnp.bfloat16)
    before = jnp.dot(earlier, owners.astype(jnp.bfloat16), preferred_element_type=jnp.float32)
    rank = jnp.sum(before * owners.astype(jnp.float32), axis=1).astype(jnp.int32)
    place = target * capacity + rank
    slots = jnp.arange(tile_count * capacity, dtype=jnp.int32)
    select = (slots[:, None] == place[None, :]).astype(hit_energy.dtype)
    send = jnp.einsum(
        "pi,ibh->pbh", select, payload, preferred_element_type=jnp.float32
    ).astype(hit_energy.dtype)
    kern = kernel_spectra(psf_bank, psf_index, K // 2)
    got = lax.all_to_all(send, "tile", split_axis=0, concat_axis=0, tiled=True)
    splat = window_splat(got, scenes)
    extended = padded_2(splat, (("tile", 2),), K // 2)
    wave_index = lax.axis_index("wave")
    my_response = lax.dynamic_slice_in_dim(response, wave_index * band_dev, band_dev, 0)
    partial = patch_blur(extended, kern, my_response, K // 2)
    color = lax.dynamic_index_in_dim(partial, wave_index, 0, keepdims=False)
    for step in range(1, wave_count):
        piece = lax.dynamic_index_in_dim(partial, (wave_index + step) % wave_count, 0, keepdims=False)
        color = color + lax.ppermute(
            piece, "wave", [(i, (i + step) % wave_count) for i in range(wave_count)]
        )
    sensor = lax.reduce_precision(color[None], exponent_bits=8, mantissa_bits=7)
    sensor = sensor.astype(jnp.bfloat16)
    rimmed = padded_2(sensor, (("tile", 2),), 2)
    hidden = jax.nn.silu(conv_rows(rimmed, conv_in))
    hidden = lax.reduce_precision(hidden, exponent_bits=8, mantissa_bits=7).astype(jnp.bfloat16)
    tile_index = lax.axis_index("tile")
    row_ids = lax.broadcasted_iota(jnp.int32, hidden.shape, 2)
    outside = ((tile_index == 0) & (row_ids == 0)) | (
        (tile_index == tile_count - 1) & (row_ids == hidden.shape[2] - 1)
    )
    hidden = jnp.where(outside, jnp.zeros_like(hidden), hidden)
    return conv_rows(hidden, conv_out).astype(jnp.bfloat16)


def solution(mesh):
    in_specs = (
        P("tile", "wave", None),
        P("wave", "tile", None),
        P("wave", "tile", None),
        P("wave", "tile"),
        P("wave", "tile"),
        P("wave", "tile"),
        P(None, "wave", None),
        P("tile", None, None),
        P(),
        P(),
        P(),
    )
    out_specs = P("wave", None, "tile", None)
    return jax.shard_map(
        per_device, mesh=mesh, in_specs=in_specs, out_specs=out_specs, check_vma=False
    )
```

```python
import functools

import jax
import jax.numpy as jnp
import numpy as np
from jax import lax
from jax.experimental import pallas as pl
from jax.sharding import PartitionSpec as P

ROWS_DEV = 16
W = 128
WIN = 4
K = 31
DFT_N = 144
LANE = 128
GROUP = 8


def padded_2(cells, sides, width):
    for axis, dim in sides:
        count = lax.axis_size(axis)
        ends = count - 1
        head = lax.slice_in_dim(cells, 0, width, axis=dim)
        tail = lax.slice_in_dim(cells, cells.shape[dim] - width, cells.shape[dim], axis=dim)
        cells = jnp.concatenate(
            [
                lax.ppermute(tail, axis, [(i, (i + 1) % count) for i in range(ends)]),
                cells,
                lax.ppermute(head, axis, [((i + 1) % count, i) for i in range(ends)]),
            ],
            axis=dim,
        )
    return cells


def conv_rows(image, weights):
    return lax.conv_general_dilated(
        image,
        weights,
        (1, 1),
        ((0, 0), (1, 1)),
        dimension_numbers=("NCHW", "OIHW", "NCHW"),
        preferred_element_type=jnp.float32,
    )


def dft_tables(width, side, radius):
    freqs = DFT_N // 2 + 1
    f = np.arange(freqs)[None, :]
    x = np.arange(width)[:, None]
    angle = 2 * np.pi * f * x / DFT_N
    forward = np.zeros((width, 2 * LANE))
    forward[:, :freqs] = np.cos(angle)
    forward[:, LANE : LANE + freqs] = -np.sin(angle)
    lag = (np.arange(side) - radius)[:, None]
    tap_angle = 2 * np.pi * f * lag / DFT_N
    taps = np.zeros((side, 2 * LANE))
    taps[:, :freqs] = np.cos(tap_angle)
    taps[:, LANE : LANE + freqs] = np.sin(tap_angle)
    weight = np.full((freqs,), 2.0)
    weight[0] = 1.0
    weight[-1] = 1.0
    back_angle = 2 * np.pi * np.arange(freqs)[:, None] * np.arange(width)[None, :] / DFT_N
    inverse = np.zeros((2 * LANE, width))
    inverse[:freqs] = weight[:, None] * np.cos(back_angle) / DFT_N
    inverse[LANE : LANE + freqs] = -weight[:, None] * np.sin(back_angle) / DFT_N
    return (
        forward.astype(np.float32),
        taps.astype(np.float32),
        inverse.astype(np.float32),
    )


def row_taps_kernel(spec_ref, kern_ref, out_ref):
    group = spec_ref.shape[0]
    side = kern_ref.shape[1]
    rows = out_ref.shape[1]

    def one(c, carry):
        acc_re = jnp.zeros((rows, LANE), jnp.float32)
        acc_im = jnp.zeros((rows, LANE), jnp.float32)
        for u in range(side):
            xr = spec_ref[c, pl.ds(u, rows), pl.ds(0, LANE)]
            xi = spec_ref[c, pl.ds(u, rows), pl.ds(LANE, LANE)]
            kr = kern_ref[c, pl.ds(u, 1), pl.ds(0, LANE)]
            ki = kern_ref[c, pl.ds(u, 1), pl.ds(LANE, LANE)]
            acc_re = acc_re + (kr * xr - ki * xi)
            acc_im = acc_im + (kr * xi + ki * xr)
        out_ref[c, :, pl.ds(0, LANE)] = acc_re
        out_ref[c, :, pl.ds(LANE, LANE)] = acc_im
        return carry

    lax.fori_loop(0, group, one, 0)


def row_taps(spec, kern, rows):
    channels, tall, both = spec.shape
    side = kern.shape[1]
    return pl.pallas_call(
        row_taps_kernel,
        out_shape=jax.ShapeDtypeStruct((channels, rows, both), jnp.float32),
        grid=(channels // GROUP,),
        in_specs=[
            pl.BlockSpec((GROUP, tall, both), lambda g: (g, 0, 0)),
            pl.BlockSpec((GROUP, side, both), lambda g: (g, 0, 0)),
        ],
        out_specs=pl.BlockSpec((GROUP, rows, both), lambda g: (g, 0, 0)),
    )(spec, kern)


def kernel_spectra(psf_bank, psf_index, radius):
    scenes = psf_index.shape[1]
    band_dev = psf_bank.shape[1]
    side = 2 * radius + 1
    unused, taps, unused_too = dft_tables(W, side, radius)
    chosen = psf_bank[psf_index[0, :, 0]].reshape(scenes, band_dev, side, side)
    return jnp.einsum("sbuv,vf->sbuf", chosen, taps, precision=lax.Precision.HIGHEST)


def patch_blur(extended, kern, response, radius):
    band_dev, scenes, tall, width = extended.shape
    rows_dev = tall - 2 * radius
    side = 2 * radius + 1
    forward, unused, inverse = dft_tables(width, side, radius)
    hi = lax.Precision.HIGHEST
    spec = jnp.einsum(
        "cyx,xf->cyf", extended.reshape(band_dev * scenes, tall, width), forward, precision=hi
    )
    taps = kern.transpose(1, 0, 2, 3).reshape(band_dev * scenes, side, -1)
    out = row_taps(spec, taps, rows_dev).reshape(band_dev, scenes, rows_dev, -1)
    color = jnp.einsum("bsyf,bc->scyf", out, response, precision=hi)
    return jnp.einsum("scyf,fx->scyx", color, inverse, precision=hi)


def window_splat(got, band_dev, hit_lanes, scenes):
    slots = got.shape[0]
    energy = got[:, : band_dev * hit_lanes].reshape(slots, band_dev, hit_lanes)
    field = got[:, band_dev * hit_lanes : (band_dev + 1) * hit_lanes].astype(jnp.int32)
    column = got[:, (band_dev + 1) * hit_lanes :].astype(jnp.int32)
    offset = field % WIN
    base = field[:, 0] // WIN
    rows = jnp.arange(WIN, dtype=jnp.int32)
    spread = jnp.where(
        offset[:, None, None, :] == rows[None, None, :, None],
        energy[:, :, None, :],
        jnp.zeros((), energy.dtype),
    )
    onehot = (column[:, :, None] == jnp.arange(W, dtype=jnp.int32)[None, None, :]).astype(
        energy.dtype
    )
    window = jnp.einsum("ibjh,ihc->ibjc", spread, onehot, preferred_element_type=jnp.float32)
    row_ids = jnp.arange(scenes * ROWS_DEV, dtype=jnp.int32)
    placing = (base[:, None, None] + rows[None, :, None] == row_ids[None, None, :]).astype(
        jnp.float32
    )
    total = jnp.einsum("ibjc,ijr->brc", window, placing, precision=lax.Precision.HIGH)
    return total.reshape(band_dev, scenes, ROWS_DEV, W)


def per_device(
    hit_energy,
    hit_spot,
    block_tile,
    block_count,
    block_scene,
    block_row,
    psf_bank,
    psf_index,
    response,
    conv_in,
    conv_out,
):
    tile_count = lax.axis_size("tile")
    wave_count = lax.axis_size("wave")
    block_dev, band_dev, hit_lanes = hit_energy.shape
    capacity = 2 * block_dev // tile_count
    scenes = psf_index.shape[1]
    lanes = lax.broadcasted_iota(jnp.int32, (block_dev, hit_lanes), 1)
    live = lanes < block_count[0][:, None]
    masked = jnp.where(live[:, None, :], hit_energy, jnp.zeros_like(hit_energy))
    base_row = block_scene[0] * ROWS_DEV + block_row[0]
    spot = hit_spot[0]
    field = base_row[:, None] * WIN + spot // W
    column = spot % W
    payload = jnp.concatenate(
        [
            masked.reshape(block_dev, band_dev * hit_lanes),
            field.astype(hit_energy.dtype),
            column.astype(hit_energy.dtype),
        ],
        axis=1,
    )
    target = block_tile[0, :, 0]
    owners = (target[:, None] == jnp.arange(tile_count, dtype=jnp.int32)[None, :]).astype(jnp.int32)
    order = lax.broadcasted_iota(jnp.int32, (block_dev, block_dev), 0)
    earlier = (order > order.T).astype(jnp.bfloat16)
    before = jnp.dot(earlier, owners.astype(jnp.bfloat16), preferred_element_type=jnp.float32)
    rank = jnp.sum(before * owners.astype(jnp.float32), axis=1).astype(jnp.int32)
    place = target * capacity + rank
    slots = jnp.arange(tile_count * capacity, dtype=jnp.int32)
    select = (slots[:, None] == place[None, :]).astype(hit_energy.dtype)
    send = jnp.dot(select, payload, preferred_element_type=jnp.float32).astype(hit_energy.dtype)
    kern = kernel_spectra(psf_bank, psf_index, K // 2)
    got = lax.all_to_all(send, "tile", split_axis=0, concat_axis=0, tiled=True)
    splat = window_splat(got, band_dev, hit_lanes, scenes)
    extended = padded_2(splat, (("tile", 2),), K // 2)
    wave_index = lax.axis_index("wave")
    my_response = lax.dynamic_slice_in_dim(response, wave_index * band_dev, band_dev, 0)
    partial = patch_blur(extended, kern, my_response, K // 2)
    color = lax.dynamic_index_in_dim(partial, wave_index, 0, keepdims=False)
    for step in range(1, wave_count):
        piece = lax.dynamic_index_in_dim(partial, (wave_index + step) % wave_count, 0, keepdims=False)
        color = color + lax.ppermute(
            piece, "wave", [(i, (i + step) % wave_count) for i in range(wave_count)]
        )
    sensor = lax.reduce_precision(color[None], exponent_bits=8, mantissa_bits=7)
    sensor = sensor.astype(jnp.bfloat16)
    rimmed = padded_2(sensor, (("tile", 2),), 2)
    hidden = jax.nn.silu(conv_rows(rimmed, conv_in))
    hidden = lax.reduce_precision(hidden, exponent_bits=8, mantissa_bits=7).astype(jnp.bfloat16)
    tile_index = lax.axis_index("tile")
    row_ids = lax.broadcasted_iota(jnp.int32, hidden.shape, 2)
    outside = ((tile_index == 0) & (row_ids == 0)) | (
        (tile_index == tile_count - 1) & (row_ids == hidden.shape[2] - 1)
    )
    hidden = jnp.where(outside, jnp.zeros_like(hidden), hidden)
    return conv_rows(hidden, conv_out).astype(jnp.bfloat16)


def solution(mesh):
    in_specs = (
        P("tile", "wave", None),
        P("wave", "tile", None),
        P("wave", "tile", None),
        P("wave", "tile"),
        P("wave", "tile"),
        P("wave", "tile"),
        P(None, "wave", None),
        P("tile", None, None),
        P(),
        P(),
        P(),
    )
    out_specs = P("wave", None, "tile", None)
    return jax.shard_map(
        per_device, mesh=mesh, in_specs=in_specs, out_specs=out_specs, check_vma=False
    )
```

```python
import functools

import jax
import jax.numpy as jnp
import numpy as np
from jax import lax
from jax.experimental import pallas as pl
from jax.sharding import PartitionSpec as P

ROWS_DEV = 16
W = 128
WIN = 4
K = 31
DFT_N = 144
LANE = 128
GROUP = 8


def padded_2(cells, sides, width):
    for axis, dim in sides:
        count = lax.axis_size(axis)
        ends = count - 1
        head = lax.slice_in_dim(cells, 0, width, axis=dim)
        tail = lax.slice_in_dim(cells, cells.shape[dim] - width, cells.shape[dim], axis=dim)
        cells = jnp.concatenate(
            [
                lax.ppermute(tail, axis, [(i, (i + 1) % count) for i in range(ends)]),
                cells,
                lax.ppermute(head, axis, [((i + 1) % count, i) for i in range(ends)]),
            ],
            axis=dim,
        )
    return cells


def conv_rows(image, weights):
    return lax.conv_general_dilated(
        image,
        weights,
        (1, 1),
        ((0, 0), (1, 1)),
        dimension_numbers=("NCHW", "OIHW", "NCHW"),
        preferred_element_type=jnp.float32,
    )


def dft_tables(width, side, radius):
    freqs = DFT_N // 2 + 1
    f = np.arange(freqs)[None, :]
    x = np.arange(width)[:, None]
    angle = 2 * np.pi * f * x / DFT_N
    forward = np.zeros((width, 2 * LANE))
    forward[:, :freqs] = np.cos(angle)
    forward[:, LANE : LANE + freqs] = -np.sin(angle)
    lag = (np.arange(side) - radius)[:, None]
    tap_angle = 2 * np.pi * f * lag / DFT_N
    taps = np.zeros((side, 2 * LANE))
    taps[:, :freqs] = np.cos(tap_angle)
    taps[:, LANE : LANE + freqs] = np.sin(tap_angle)
    weight = np.full((freqs,), 2.0)
    weight[0] = 1.0
    weight[-1] = 1.0
    back_angle = 2 * np.pi * np.arange(freqs)[:, None] * np.arange(width)[None, :] / DFT_N
    inverse = np.zeros((2 * LANE, width))
    inverse[:freqs] = weight[:, None] * np.cos(back_angle) / DFT_N
    inverse[LANE : LANE + freqs] = -weight[:, None] * np.sin(back_angle) / DFT_N
    return (
        forward.astype(np.float32),
        taps.astype(np.float32),
        inverse.astype(np.float32),
    )


def row_taps_kernel(spec_ref, kern_ref, out_ref):
    group = spec_ref.shape[0]
    side = kern_ref.shape[1]
    rows = out_ref.shape[1]

    def one(c, carry):
        acc_re = jnp.zeros((rows, LANE), jnp.float32)
        acc_im = jnp.zeros((rows, LANE), jnp.float32)
        for u in range(side):
            xr = spec_ref[c, pl.ds(u, rows), pl.ds(0, LANE)]
            xi = spec_ref[c, pl.ds(u, rows), pl.ds(LANE, LANE)]
            kr = kern_ref[c, pl.ds(u, 1), pl.ds(0, LANE)]
            ki = kern_ref[c, pl.ds(u, 1), pl.ds(LANE, LANE)]
            acc_re = acc_re + (kr * xr - ki * xi)
            acc_im = acc_im + (kr * xi + ki * xr)
        out_ref[c, :, pl.ds(0, LANE)] = acc_re
        out_ref[c, :, pl.ds(LANE, LANE)] = acc_im
        return carry

    lax.fori_loop(0, group, one, 0)


def row_taps(spec, kern, rows):
    channels, tall, both = spec.shape
    side = kern.shape[1]
    return pl.pallas_call(
        row_taps_kernel,
        out_shape=jax.ShapeDtypeStruct((channels, rows, both), jnp.float32),
        grid=(channels // GROUP,),
        in_specs=[
            pl.BlockSpec((GROUP, tall, both), lambda g: (g, 0, 0)),
            pl.BlockSpec((GROUP, side, both), lambda g: (g, 0, 0)),
        ],
        out_specs=pl.BlockSpec((GROUP, rows, both), lambda g: (g, 0, 0)),
    )(spec, kern)


def kernel_spectra(psf_bank, psf_index, radius):
    scenes = psf_index.shape[1]
    band_dev = psf_bank.shape[1]
    side = 2 * radius + 1
    unused, taps, unused_too = dft_tables(W, side, radius)
    chosen = psf_bank[psf_index[0, :, 0]].reshape(scenes, band_dev, side, side)
    return jnp.einsum("sbuv,vf->sbuf", chosen, taps, precision=lax.Precision.HIGHEST)


def patch_blur(extended, kern, response, radius):
    band_dev, scenes, tall, width = extended.shape
    rows_dev = tall - 2 * radius
    side = 2 * radius + 1
    forward, unused, inverse = dft_tables(width, side, radius)
    hi = lax.Precision.HIGHEST
    spec = jnp.einsum(
        "cyx,xf->cyf", extended.reshape(band_dev * scenes, tall, width), forward, precision=hi
    )
    taps = kern.transpose(1, 0, 2, 3).reshape(band_dev * scenes, side, -1)
    out = row_taps(spec, taps, rows_dev).reshape(band_dev, scenes, rows_dev, -1)
    color = jnp.einsum("bsyf,bc->scyf", out, response, precision=hi)
    return jnp.einsum("scyf,fx->scyx", color, inverse, precision=hi)


def window_splat(got, band_dev, hit_lanes, scenes):
    slots = got.shape[0]
    energy = got[:, : band_dev * hit_lanes].reshape(slots, band_dev, hit_lanes)
    field = got[:, band_dev * hit_lanes : (band_dev + 1) * hit_lanes].astype(jnp.int32)
    column = got[:, (band_dev + 1) * hit_lanes :].astype(jnp.int32)
    offset = field % WIN
    base = field[:, 0] // WIN
    rows = jnp.arange(WIN, dtype=jnp.int32)
    spread = jnp.where(
        offset[:, None, None, :] == rows[None, None, :, None],
        energy[:, :, None, :],
        jnp.zeros((), energy.dtype),
    )
    onehot = (column[:, :, None] == jnp.arange(W, dtype=jnp.int32)[None, None, :]).astype(
        energy.dtype
    )
    window = jnp.einsum("ibjh,ihc->ibjc", spread, onehot, preferred_element_type=jnp.float32)
    row_ids = jnp.arange(scenes * ROWS_DEV, dtype=jnp.int32)
    placing = (base[:, None, None] + rows[None, :, None] == row_ids[None, None, :]).astype(
        jnp.float32
    )
    total = jnp.einsum("ibjc,ijr->brc", window, placing, precision=lax.Precision.HIGH)
    return total.reshape(band_dev, scenes, ROWS_DEV, W)


def per_device(
    hit_energy,
    hit_spot,
    block_tile,
    block_count,
    block_scene,
    block_row,
    psf_bank,
    psf_index,
    response,
    conv_in,
    conv_out,
):
    tile_count = lax.axis_size("tile")
    wave_count = lax.axis_size("wave")
    block_dev, band_dev, hit_lanes = hit_energy.shape
    capacity = 2 * block_dev // tile_count
    scenes = psf_index.shape[1]
    lanes = lax.broadcasted_iota(jnp.int32, (block_dev, hit_lanes), 1)
    live = lanes < block_count[0][:, None]
    masked = jnp.where(live[:, None, :], hit_energy, jnp.zeros_like(hit_energy))
    base_row = block_scene[0] * ROWS_DEV + block_row[0]
    spot = hit_spot[0]
    field = base_row[:, None] * WIN + spot // W
    column = spot % W
    payload = jnp.concatenate(
        [
            masked.reshape(block_dev, band_dev * hit_lanes),
            field.astype(hit_energy.dtype),
            column.astype(hit_energy.dtype),
        ],
        axis=1,
    )
    target = block_tile[0, :, 0]
    owners = (target[:, None] == jnp.arange(tile_count, dtype=jnp.int32)[None, :]).astype(jnp.int32)
    order = lax.broadcasted_iota(jnp.int32, (block_dev, block_dev), 0)
    earlier = (order > order.T).astype(jnp.bfloat16)
    before = jnp.dot(earlier, owners.astype(jnp.bfloat16), preferred_element_type=jnp.float32)
    rank = jnp.sum(before * owners.astype(jnp.float32), axis=1).astype(jnp.int32)
    place = target * capacity + rank
    slots = jnp.arange(tile_count * capacity, dtype=jnp.int32)
    select = (slots[:, None] == place[None, :]).astype(hit_energy.dtype)
    send = jnp.dot(select, payload, preferred_element_type=jnp.float32).astype(hit_energy.dtype)
    kern = kernel_spectra(psf_bank, psf_index, K // 2)
    got = lax.all_to_all(send, "tile", split_axis=0, concat_axis=0, tiled=True)
    splat = window_splat(got, band_dev, hit_lanes, scenes)
    extended = padded_2(splat, (("tile", 2),), K // 2)
    wave_index = lax.axis_index("wave")
    my_response = lax.dynamic_slice_in_dim(response, wave_index * band_dev, band_dev, 0)
    partial = patch_blur(extended, kern, my_response, K // 2)
    if wave_count == 4:
        far = [(i, i ^ 2) for i in range(4)]
        near = [(i, i ^ 1) for i in range(4)]
        pairs = partial.reshape(2, 2, *partial.shape[1:])
        mine = lax.dynamic_index_in_dim(pairs, wave_index // 2, 0, keepdims=False)
        theirs = lax.dynamic_index_in_dim(pairs, 1 - wave_index // 2, 0, keepdims=False)
        half = mine + lax.ppermute(theirs, "wave", far)
        own = lax.dynamic_index_in_dim(half, wave_index % 2, 0, keepdims=False)
        other = lax.dynamic_index_in_dim(half, 1 - wave_index % 2, 0, keepdims=False)
        color = own + lax.ppermute(other, "wave", near)
    else:
        color = lax.dynamic_index_in_dim(partial, wave_index, 0, keepdims=False)
        for step in range(1, wave_count):
            piece = lax.dynamic_index_in_dim(
                partial, (wave_index + step) % wave_count, 0, keepdims=False
            )
            color = color + lax.ppermute(
                piece, "wave", [(i, (i + step) % wave_count) for i in range(wave_count)]
            )
    sensor = lax.reduce_precision(color[None], exponent_bits=8, mantissa_bits=7)
    sensor = sensor.astype(jnp.bfloat16)
    rimmed = padded_2(sensor, (("tile", 2),), 2)
    hidden = jax.nn.silu(conv_rows(rimmed, conv_in))
    hidden = lax.reduce_precision(hidden, exponent_bits=8, mantissa_bits=7).astype(jnp.bfloat16)
    tile_index = lax.axis_index("tile")
    row_ids = lax.broadcasted_iota(jnp.int32, hidden.shape, 2)
    outside = ((tile_index == 0) & (row_ids == 0)) | (
        (tile_index == tile_count - 1) & (row_ids == hidden.shape[2] - 1)
    )
    hidden = jnp.where(outside, jnp.zeros_like(hidden), hidden)
    return conv_rows(hidden, conv_out).astype(jnp.bfloat16)


def solution(mesh):
    in_specs = (
        P("tile", "wave", None),
        P("wave", "tile", None),
        P("wave", "tile", None),
        P("wave", "tile"),
        P("wave", "tile"),
        P("wave", "tile"),
        P(None, "wave", None),
        P("tile", None, None),
        P(),
        P(),
        P(),
    )
    out_specs = P("wave", None, "tile", None)
    return jax.shard_map(
        per_device, mesh=mesh, in_specs=in_specs, out_specs=out_specs, check_vma=False
    )
```

```python
import functools

import jax
import jax.numpy as jnp
import numpy as np
from jax import lax
from jax.experimental import pallas as pl
from jax.sharding import PartitionSpec as P

ROWS_DEV = 16
W = 128
WIN = 4
K = 31
DFT_N = 144
LANE = 128
GROUP = 8


def padded_2(cells, sides, width):
    for axis, dim in sides:
        count = lax.axis_size(axis)
        ends = count - 1
        head = lax.slice_in_dim(cells, 0, width, axis=dim)
        tail = lax.slice_in_dim(cells, cells.shape[dim] - width, cells.shape[dim], axis=dim)
        cells = jnp.concatenate(
            [
                lax.ppermute(tail, axis, [(i, (i + 1) % count) for i in range(ends)]),
                cells,
                lax.ppermute(head, axis, [((i + 1) % count, i) for i in range(ends)]),
            ],
            axis=dim,
        )
    return cells


def conv_rows(image, weights):
    return lax.conv_general_dilated(
        image,
        weights,
        (1, 1),
        ((0, 0), (1, 1)),
        dimension_numbers=("NCHW", "OIHW", "NCHW"),
        preferred_element_type=jnp.float32,
    )


def dft_tables(width, side, radius):
    freqs = DFT_N // 2 + 1
    f = np.arange(freqs)[None, :]
    x = np.arange(width)[:, None]
    angle = 2 * np.pi * f * x / DFT_N
    forward = np.zeros((width, 2 * LANE))
    forward[:, :freqs] = np.cos(angle)
    forward[:, LANE : LANE + freqs] = -np.sin(angle)
    lag = (np.arange(side) - radius)[:, None]
    tap_angle = 2 * np.pi * f * lag / DFT_N
    taps = np.zeros((side, 2 * LANE))
    taps[:, :freqs] = np.cos(tap_angle)
    taps[:, LANE : LANE + freqs] = np.sin(tap_angle)
    weight = np.full((freqs,), 2.0)
    weight[0] = 1.0
    weight[-1] = 1.0
    back_angle = 2 * np.pi * np.arange(freqs)[:, None] * np.arange(width)[None, :] / DFT_N
    inverse = np.zeros((2 * LANE, width))
    inverse[:freqs] = weight[:, None] * np.cos(back_angle) / DFT_N
    inverse[LANE : LANE + freqs] = -weight[:, None] * np.sin(back_angle) / DFT_N
    return (
        forward.astype(np.float32),
        taps.astype(np.float32),
        inverse.astype(np.float32),
    )


def row_taps_kernel(spec_ref, kern_ref, out_ref):
    group = spec_ref.shape[0]
    side = kern_ref.shape[1]
    rows = out_ref.shape[1]

    def one(c, carry):
        acc_re = jnp.zeros((rows, LANE), jnp.float32)
        acc_im = jnp.zeros((rows, LANE), jnp.float32)
        for u in range(side):
            xr = spec_ref[c, pl.ds(u, rows), pl.ds(0, LANE)]
            xi = spec_ref[c, pl.ds(u, rows), pl.ds(LANE, LANE)]
            kr = kern_ref[c, pl.ds(u, 1), pl.ds(0, LANE)]
            ki = kern_ref[c, pl.ds(u, 1), pl.ds(LANE, LANE)]
            acc_re = acc_re + (kr * xr - ki * xi)
            acc_im = acc_im + (kr * xi + ki * xr)
        out_ref[c, :, pl.ds(0, LANE)] = acc_re
        out_ref[c, :, pl.ds(LANE, LANE)] = acc_im
        return carry

    lax.fori_loop(0, group, one, 0)


def row_taps(spec, kern, rows):
    channels, tall, both = spec.shape
    side = kern.shape[1]
    return pl.pallas_call(
        row_taps_kernel,
        out_shape=jax.ShapeDtypeStruct((channels, rows, both), jnp.float32),
        grid=(channels // GROUP,),
        in_specs=[
            pl.BlockSpec((GROUP, tall, both), lambda g: (g, 0, 0)),
            pl.BlockSpec((GROUP, side, both), lambda g: (g, 0, 0)),
        ],
        out_specs=pl.BlockSpec((GROUP, rows, both), lambda g: (g, 0, 0)),
    )(spec, kern)


def kernel_spectra(psf_bank, psf_index, radius):
    scenes = psf_index.shape[1]
    band_dev = psf_bank.shape[1]
    side = 2 * radius + 1
    unused, taps, unused_too = dft_tables(W, side, radius)
    chosen = psf_bank[psf_index[0, :, 0]].reshape(scenes, band_dev, side, side)
    return jnp.einsum("sbuv,vf->sbuf", chosen, taps, precision=lax.Precision.HIGHEST)


def patch_blur(extended, kern, response, radius):
    band_dev, scenes, tall, width = extended.shape
    rows_dev = tall - 2 * radius
    side = 2 * radius + 1
    forward, unused, inverse = dft_tables(width, side, radius)
    hi = lax.Precision.HIGHEST
    spec = jnp.einsum(
        "cyx,xf->cyf", extended.reshape(band_dev * scenes, tall, width), forward, precision=hi
    )
    taps = kern.transpose(1, 0, 2, 3).reshape(band_dev * scenes, side, -1)
    out = row_taps(spec, taps, rows_dev).reshape(band_dev, scenes, rows_dev, -1)
    color = jnp.einsum("bsyf,bc->scyf", out, response, precision=hi)
    return jnp.einsum("scyf,fx->scyx", color, inverse, precision=hi)


def window_splat(got, band_dev, hit_lanes, scenes):
    slots = got.shape[0]
    energy = got[:, : band_dev * hit_lanes].reshape(slots, band_dev, hit_lanes)
    field = got[:, band_dev * hit_lanes : (band_dev + 1) * hit_lanes].astype(jnp.int32)
    column = got[:, (band_dev + 1) * hit_lanes :].astype(jnp.int32)
    offset = field % WIN
    base = field[:, 0] // WIN
    rows = jnp.arange(WIN, dtype=jnp.int32)
    spread = jnp.where(
        offset[:, None, None, :] == rows[None, None, :, None],
        energy[:, :, None, :],
        jnp.zeros((), energy.dtype),
    )
    onehot = (column[:, :, None] == jnp.arange(W, dtype=jnp.int32)[None, None, :]).astype(
        energy.dtype
    )
    window = jnp.einsum("ibjh,ihc->ibjc", spread, onehot, preferred_element_type=jnp.float32)
    row_ids = jnp.arange(scenes * ROWS_DEV, dtype=jnp.int32)
    placing = (base[:, None, None] + rows[None, :, None] == row_ids[None, None, :]).astype(
        jnp.float32
    )
    total = jnp.einsum("ibjc,ijr->brc", window, placing, precision=lax.Precision.HIGH)
    return total.reshape(band_dev, scenes, ROWS_DEV, W)


def pack_kernel(capacity, energy_ref, spot_ref, tile_ref, count_ref, scene_ref, row_ref, out_ref):
    blocks, width = energy_ref.shape
    hits = spot_ref.shape[1]
    slots = out_ref.shape[0]
    tiles = slots // capacity
    f32 = jnp.float32
    ii = lax.broadcasted_iota(jnp.int32, (blocks, blocks), 0)
    jj = lax.broadcasted_iota(jnp.int32, (blocks, blocks), 1)
    eye = ii == jj
    tile_row = tile_ref[...].astype(f32)
    count_row = count_ref[...].astype(f32)
    base_row = (scene_ref[...] * ROWS_DEV + row_ref[...]).astype(f32)
    zero = jnp.zeros((blocks, blocks), f32)
    count_col = jnp.sum(jnp.where(eye, count_row, zero), axis=1, keepdims=True)
    base_col = jnp.sum(jnp.where(eye, base_row, zero), axis=1, keepdims=True)
    lanes = lax.broadcasted_iota(jnp.int32, (blocks, width), 1) % hits
    live = lanes.astype(f32) < count_col
    energy = energy_ref[...]
    masked = jnp.where(live, energy, jnp.zeros_like(energy))
    spot = spot_ref[...]
    field = base_col * WIN + lax.shift_right_logical(spot, 7).astype(f32)
    column = jnp.bitwise_and(spot, W - 1).astype(f32)
    tt = lax.broadcasted_iota(jnp.int32, (tiles, blocks), 0).astype(f32)
    owners = (tt == tile_row).astype(jnp.bfloat16)
    earlier = (ii < jj).astype(jnp.bfloat16)
    before = jnp.dot(owners, earlier, preferred_element_type=f32)
    rank = jnp.sum(before * owners.astype(f32), axis=0, keepdims=True)
    place = tile_row * capacity + rank
    pp = lax.broadcasted_iota(jnp.int32, (slots, blocks), 0).astype(f32)
    select = (pp == place).astype(jnp.bfloat16)
    out_ref[:, pl.ds(0, width)] = jnp.dot(select, masked, preferred_element_type=f32).astype(
        out_ref.dtype
    )
    out_ref[:, pl.ds(width, hits)] = jnp.dot(
        select, field.astype(jnp.bfloat16), preferred_element_type=f32
    ).astype(out_ref.dtype)
    out_ref[:, pl.ds(width + hits, hits)] = jnp.dot(
        select, column.astype(jnp.bfloat16), preferred_element_type=f32
    ).astype(out_ref.dtype)


def pack(energy, spot, tile, count, scene, row, capacity, slots):
    blocks, width = energy.shape
    hits = spot.shape[1]
    return pl.pallas_call(
        functools.partial(pack_kernel, capacity),
        out_shape=jax.ShapeDtypeStruct((slots, width + 2 * hits), energy.dtype),
    )(energy, spot, tile, count, scene, row)


def per_device(
    hit_energy,
    hit_spot,
    block_tile,
    block_count,
    block_scene,
    block_row,
    psf_bank,
    psf_index,
    response,
    conv_in,
    conv_out,
):
    tile_count = lax.axis_size("tile")
    wave_count = lax.axis_size("wave")
    block_dev, band_dev, hit_lanes = hit_energy.shape
    capacity = 2 * block_dev // tile_count
    scenes = psf_index.shape[1]
    send = pack(
        hit_energy.reshape(block_dev, band_dev * hit_lanes),
        hit_spot[0],
        block_tile[0, :, 0].reshape(1, block_dev),
        block_count,
        block_scene,
        block_row,
        capacity,
        tile_count * capacity,
    )
    kern = kernel_spectra(psf_bank, psf_index, K // 2)
    got = lax.all_to_all(send, "tile", split_axis=0, concat_axis=0, tiled=True)
    splat = window_splat(got, band_dev, hit_lanes, scenes)
    extended = padded_2(splat, (("tile", 2),), K // 2)
    wave_index = lax.axis_index("wave")
    my_response = lax.dynamic_slice_in_dim(response, wave_index * band_dev, band_dev, 0)
    partial = patch_blur(extended, kern, my_response, K // 2)
    color = lax.dynamic_index_in_dim(partial, wave_index, 0, keepdims=False)
    for step in range(1, wave_count):
        piece = lax.dynamic_index_in_dim(partial, (wave_index + step) % wave_count, 0, keepdims=False)
        color = color + lax.ppermute(
            piece, "wave", [(i, (i + step) % wave_count) for i in range(wave_count)]
        )
    sensor = lax.reduce_precision(color[None], exponent_bits=8, mantissa_bits=7)
    sensor = sensor.astype(jnp.bfloat16)
    rimmed = padded_2(sensor, (("tile", 2),), 2)
    hidden = jax.nn.silu(conv_rows(rimmed, conv_in))
    hidden = lax.reduce_precision(hidden, exponent_bits=8, mantissa_bits=7).astype(jnp.bfloat16)
    tile_index = lax.axis_index("tile")
    row_ids = lax.broadcasted_iota(jnp.int32, hidden.shape, 2)
    outside = ((tile_index == 0) & (row_ids == 0)) | (
        (tile_index == tile_count - 1) & (row_ids == hidden.shape[2] - 1)
    )
    hidden = jnp.where(outside, jnp.zeros_like(hidden), hidden)
    return conv_rows(hidden, conv_out).astype(jnp.bfloat16)


def solution(mesh):
    in_specs = (
        P("tile", "wave", None),
        P("wave", "tile", None),
        P("wave", "tile", None),
        P("wave", "tile"),
        P("wave", "tile"),
        P("wave", "tile"),
        P(None, "wave", None),
        P("tile", None, None),
        P(),
        P(),
        P(),
    )
    out_specs = P("wave", None, "tile", None)
    return jax.shard_map(
        per_device, mesh=mesh, in_specs=in_specs, out_specs=out_specs, check_vma=False
    )
```

```python
import functools

import jax
import jax.numpy as jnp
import numpy as np
from jax import lax
from jax.experimental import pallas as pl
from jax.experimental.pallas import tpu as pltpu
from jax.sharding import PartitionSpec as P

ROWS_DEV = 16
W = 128
WIN = 4
K = 31
DFT_N = 144
LANE = 128
GROUP = 8


def padded_2(cells, sides, width):
    for axis, dim in sides:
        count = lax.axis_size(axis)
        ends = count - 1
        head = lax.slice_in_dim(cells, 0, width, axis=dim)
        tail = lax.slice_in_dim(cells, cells.shape[dim] - width, cells.shape[dim], axis=dim)
        cells = jnp.concatenate(
            [
                lax.ppermute(tail, axis, [(i, (i + 1) % count) for i in range(ends)]),
                cells,
                lax.ppermute(head, axis, [((i + 1) % count, i) for i in range(ends)]),
            ],
            axis=dim,
        )
    return cells


def conv_rows(image, weights):
    return lax.conv_general_dilated(
        image,
        weights,
        (1, 1),
        ((0, 0), (1, 1)),
        dimension_numbers=("NCHW", "OIHW", "NCHW"),
        preferred_element_type=jnp.float32,
    )


def dft_tables(width, side, radius):
    freqs = DFT_N // 2 + 1
    f = np.arange(freqs)[None, :]
    x = np.arange(width)[:, None]
    angle = 2 * np.pi * f * x / DFT_N
    forward = np.zeros((width, 2 * LANE))
    forward[:, :freqs] = np.cos(angle)
    forward[:, LANE : LANE + freqs] = -np.sin(angle)
    lag = (np.arange(side) - radius)[:, None]
    tap_angle = 2 * np.pi * f * lag / DFT_N
    taps = np.zeros((side, 2 * LANE))
    taps[:, :freqs] = np.cos(tap_angle)
    taps[:, LANE : LANE + freqs] = np.sin(tap_angle)
    weight = np.full((freqs,), 2.0)
    weight[0] = 1.0
    weight[-1] = 1.0
    back_angle = 2 * np.pi * np.arange(freqs)[:, None] * np.arange(width)[None, :] / DFT_N
    inverse = np.zeros((2 * LANE, width))
    inverse[:freqs] = weight[:, None] * np.cos(back_angle) / DFT_N
    inverse[LANE : LANE + freqs] = -weight[:, None] * np.sin(back_angle) / DFT_N
    return (
        forward.astype(np.float32),
        taps.astype(np.float32),
        inverse.astype(np.float32),
    )


def row_taps_kernel(spec_ref, kern_ref, out_ref):
    group = spec_ref.shape[0]
    side = kern_ref.shape[1]
    rows = out_ref.shape[1]

    def one(c, carry):
        acc_re = jnp.zeros((rows, LANE), jnp.float32)
        acc_im = jnp.zeros((rows, LANE), jnp.float32)
        for u in range(side):
            xr = spec_ref[c, pl.ds(u, rows), pl.ds(0, LANE)]
            xi = spec_ref[c, pl.ds(u, rows), pl.ds(LANE, LANE)]
            kr = kern_ref[c, pl.ds(u, 1), pl.ds(0, LANE)]
            ki = kern_ref[c, pl.ds(u, 1), pl.ds(LANE, LANE)]
            acc_re = acc_re + (kr * xr - ki * xi)
            acc_im = acc_im + (kr * xi + ki * xr)
        out_ref[c, :, pl.ds(0, LANE)] = acc_re
        out_ref[c, :, pl.ds(LANE, LANE)] = acc_im
        return carry

    lax.fori_loop(0, group, one, 0)


def row_taps(spec, kern, rows):
    channels, tall, both = spec.shape
    side = kern.shape[1]
    return pl.pallas_call(
        row_taps_kernel,
        out_shape=jax.ShapeDtypeStruct((channels, rows, both), jnp.float32),
        grid=(channels // GROUP,),
        in_specs=[
            pl.BlockSpec((GROUP, tall, both), lambda g: (g, 0, 0)),
            pl.BlockSpec((GROUP, side, both), lambda g: (g, 0, 0)),
        ],
        out_specs=pl.BlockSpec((GROUP, rows, both), lambda g: (g, 0, 0)),
    )(spec, kern)


def kernel_spectra(psf_bank, psf_index, radius):
    scenes = psf_index.shape[1]
    band_dev = psf_bank.shape[1]
    side = 2 * radius + 1
    unused, taps, unused_too = dft_tables(W, side, radius)
    chosen = psf_bank[psf_index[0, :, 0]].reshape(scenes, band_dev, side, side)
    return jnp.einsum("sbuv,vf->sbuf", chosen, taps, precision=lax.Precision.HIGHEST)


def blur_kernel(ext_ref, fwd_ref, kern_ref, resp_ref, inv_ref, out_ref, spec_scr, col_scr):
    step = pl.program_id(0)
    per = ext_ref.shape[0]
    scenes, colors, rows = out_ref.shape[:3]
    side = kern_ref.shape[1]
    group = per // scenes
    hi = lax.Precision.HIGHEST

    @pl.when(step == 0)
    def _():
        col_scr[...] = jnp.zeros_like(col_scr)

    def band(g, carry):
        b = step * group + g
        for s in range(scenes):
            c = g * scenes + s
            spec_scr[...] = jnp.dot(
                ext_ref[c], fwd_ref[...], precision=hi, preferred_element_type=jnp.float32
            )
            acc_re = jnp.zeros((rows, LANE), jnp.float32)
            acc_im = jnp.zeros((rows, LANE), jnp.float32)
            for u in range(side):
                xr = spec_scr[pl.ds(u, rows), pl.ds(0, LANE)]
                xi = spec_scr[pl.ds(u, rows), pl.ds(LANE, LANE)]
                kr = kern_ref[c, pl.ds(u, 1), pl.ds(0, LANE)]
                ki = kern_ref[c, pl.ds(u, 1), pl.ds(LANE, LANE)]
                acc_re = acc_re + (kr * xr - ki * xi)
                acc_im = acc_im + (kr * xi + ki * xr)
            for k in range(colors):
                weight = resp_ref[b, k]
                col_scr[s, k, :, pl.ds(0, LANE)] += weight * acc_re
                col_scr[s, k, :, pl.ds(LANE, LANE)] += weight * acc_im
        return carry

    lax.fori_loop(0, group, band, 0)

    @pl.when(step == pl.num_programs(0) - 1)
    def _():
        for s in range(scenes):
            for k in range(colors):
                out_ref[s, k] = jnp.dot(
                    col_scr[s, k], inv_ref[...], precision=hi, preferred_element_type=jnp.float32
                )


def patch_blur(extended, kern, response, radius):
    band_dev, scenes, tall, width = extended.shape
    rows_dev = tall - 2 * radius
    side = 2 * radius + 1
    colors = response.shape[1]
    forward, unused, inverse = dft_tables(width, side, radius)
    taps = kern.transpose(1, 0, 2, 3).reshape(band_dev * scenes, side, -1)
    both = taps.shape[-1]
    group = 4 if band_dev % 4 == 0 else 1
    per = group * scenes
    return pl.pallas_call(
        blur_kernel,
        out_shape=jax.ShapeDtypeStruct((scenes, colors, rows_dev, width), jnp.float32),
        grid=(band_dev // group,),
        in_specs=[
            pl.BlockSpec((per, tall, width), lambda i: (i, 0, 0)),
            pl.BlockSpec((width, both), lambda i: (0, 0)),
            pl.BlockSpec((per, side, both), lambda i: (i, 0, 0)),
            pl.BlockSpec(memory_space=pltpu.SMEM),
            pl.BlockSpec((both, width), lambda i: (0, 0)),
        ],
        out_specs=pl.BlockSpec((scenes, colors, rows_dev, width), lambda i: (0, 0, 0, 0)),
        scratch_shapes=[
            pltpu.VMEM((tall, both), jnp.float32),
            pltpu.VMEM((scenes, colors, rows_dev, both), jnp.float32),
        ],
    )(
        extended.reshape(band_dev * scenes, tall, width),
        jnp.asarray(forward),
        taps,
        response,
        jnp.asarray(inverse),
    )


def window_splat(got, band_dev, hit_lanes, scenes):
    slots = got.shape[0]
    energy = got[:, : band_dev * hit_lanes].reshape(slots, band_dev, hit_lanes)
    field = got[:, band_dev * hit_lanes : (band_dev + 1) * hit_lanes].astype(jnp.int32)
    column = got[:, (band_dev + 1) * hit_lanes :].astype(jnp.int32)
    offset = field % WIN
    base = field[:, 0] // WIN
    rows = jnp.arange(WIN, dtype=jnp.int32)
    spread = jnp.where(
        offset[:, None, None, :] == rows[None, None, :, None],
        energy[:, :, None, :],
        jnp.zeros((), energy.dtype),
    )
    onehot = (column[:, :, None] == jnp.arange(W, dtype=jnp.int32)[None, None, :]).astype(
        energy.dtype
    )
    window = jnp.einsum("ibjh,ihc->ibjc", spread, onehot, preferred_element_type=jnp.float32)
    row_ids = jnp.arange(scenes * ROWS_DEV, dtype=jnp.int32)
    placing = (base[:, None, None] + rows[None, :, None] == row_ids[None, None, :]).astype(
        jnp.float32
    )
    total = jnp.einsum("ibjc,ijr->brc", window, placing, precision=lax.Precision.HIGH)
    return total.reshape(band_dev, scenes, ROWS_DEV, W)


def pack_kernel(capacity, energy_ref, spot_ref, tile_ref, count_ref, scene_ref, row_ref, out_ref):
    blocks, width = energy_ref.shape
    hits = spot_ref.shape[1]
    slots = out_ref.shape[0]
    tiles = slots // capacity
    f32 = jnp.float32
    ii = lax.broadcasted_iota(jnp.int32, (blocks, blocks), 0)
    jj = lax.broadcasted_iota(jnp.int32, (blocks, blocks), 1)
    eye = ii == jj
    tile_row = tile_ref[...].astype(f32)
    count_row = count_ref[...].astype(f32)
    base_row = (scene_ref[...] * ROWS_DEV + row_ref[...]).astype(f32)
    zero = jnp.zeros((blocks, blocks), f32)
    count_col = jnp.sum(jnp.where(eye, count_row, zero), axis=1, keepdims=True)
    base_col = jnp.sum(jnp.where(eye, base_row, zero), axis=1, keepdims=True)
    lanes = lax.broadcasted_iota(jnp.int32, (blocks, width), 1) % hits
    live = lanes.astype(f32) < count_col
    energy = energy_ref[...]
    masked = jnp.where(live, energy, jnp.zeros_like(energy))
    spot = spot_ref[...]
    field = base_col * WIN + lax.shift_right_logical(spot, 7).astype(f32)
    column = jnp.bitwise_and(spot, W - 1).astype(f32)
    tt = lax.broadcasted_iota(jnp.int32, (tiles, blocks), 0).astype(f32)
    owners = (tt == tile_row).astype(jnp.bfloat16)
    earlier = (ii < jj).astype(jnp.bfloat16)
    before = jnp.dot(owners, earlier, preferred_element_type=f32)
    rank = jnp.sum(before * owners.astype(f32), axis=0, keepdims=True)
    place = tile_row * capacity + rank
    pp = lax.broadcasted_iota(jnp.int32, (slots, blocks), 0).astype(f32)
    select = (pp == place).astype(jnp.bfloat16)
    out_ref[:, pl.ds(0, width)] = jnp.dot(select, masked, preferred_element_type=f32).astype(
        out_ref.dtype
    )
    out_ref[:, pl.ds(width, hits)] = jnp.dot(
        select, field.astype(jnp.bfloat16), preferred_element_type=f32
    ).astype(out_ref.dtype)
    out_ref[:, pl.ds(width + hits, hits)] = jnp.dot(
        select, column.astype(jnp.bfloat16), preferred_element_type=f32
    ).astype(out_ref.dtype)


def pack(energy, spot, tile, count, scene, row, capacity, slots):
    blocks, width = energy.shape
    hits = spot.shape[1]
    return pl.pallas_call(
        functools.partial(pack_kernel, capacity),
        out_shape=jax.ShapeDtypeStruct((slots, width + 2 * hits), energy.dtype),
    )(energy, spot, tile, count, scene, row)


def per_device(
    hit_energy,
    hit_spot,
    block_tile,
    block_count,
    block_scene,
    block_row,
    psf_bank,
    psf_index,
    response,
    conv_in,
    conv_out,
):
    tile_count = lax.axis_size("tile")
    wave_count = lax.axis_size("wave")
    block_dev, band_dev, hit_lanes = hit_energy.shape
    capacity = 2 * block_dev // tile_count
    scenes = psf_index.shape[1]
    send = pack(
        hit_energy.reshape(block_dev, band_dev * hit_lanes),
        hit_spot[0],
        block_tile[0, :, 0].reshape(1, block_dev),
        block_count,
        block_scene,
        block_row,
        capacity,
        tile_count * capacity,
    )
    kern = kernel_spectra(psf_bank, psf_index, K // 2)
    got = lax.all_to_all(send, "tile", split_axis=0, concat_axis=0, tiled=True)
    splat = window_splat(got, band_dev, hit_lanes, scenes)
    extended = padded_2(splat, (("tile", 2),), K // 2)
    wave_index = lax.axis_index("wave")
    my_response = lax.dynamic_slice_in_dim(response, wave_index * band_dev, band_dev, 0)
    partial = patch_blur(extended, kern, my_response, K // 2)
    color = lax.dynamic_index_in_dim(partial, wave_index, 0, keepdims=False)
    for step in range(1, wave_count):
        piece = lax.dynamic_index_in_dim(partial, (wave_index + step) % wave_count, 0, keepdims=False)
        color = color + lax.ppermute(
            piece, "wave", [(i, (i + step) % wave_count) for i in range(wave_count)]
        )
    sensor = lax.reduce_precision(color[None], exponent_bits=8, mantissa_bits=7)
    sensor = sensor.astype(jnp.bfloat16)
    rimmed = padded_2(sensor, (("tile", 2),), 2)
    hidden = jax.nn.silu(conv_rows(rimmed, conv_in))
    hidden = lax.reduce_precision(hidden, exponent_bits=8, mantissa_bits=7).astype(jnp.bfloat16)
    tile_index = lax.axis_index("tile")
    row_ids = lax.broadcasted_iota(jnp.int32, hidden.shape, 2)
    outside = ((tile_index == 0) & (row_ids == 0)) | (
        (tile_index == tile_count - 1) & (row_ids == hidden.shape[2] - 1)
    )
    hidden = jnp.where(outside, jnp.zeros_like(hidden), hidden)
    return conv_rows(hidden, conv_out).astype(jnp.bfloat16)


def solution(mesh):
    in_specs = (
        P("tile", "wave", None),
        P("wave", "tile", None),
        P("wave", "tile", None),
        P("wave", "tile"),
        P("wave", "tile"),
        P("wave", "tile"),
        P(None, "wave", None),
        P("tile", None, None),
        P(),
        P(),
        P(),
    )
    out_specs = P("wave", None, "tile", None)
    return jax.shard_map(
        per_device, mesh=mesh, in_specs=in_specs, out_specs=out_specs, check_vma=False
    )
```

```python
import functools

import jax
import jax.numpy as jnp
import numpy as np
from jax import lax
from jax.experimental import pallas as pl
from jax.sharding import PartitionSpec as P

ROWS_DEV = 16
W = 128
WIN = 4
K = 31
DFT_N = 144
LANE = 128
GROUP = 8


def padded_2(cells, sides, width):
    for axis, dim in sides:
        count = lax.axis_size(axis)
        ends = count - 1
        head = lax.slice_in_dim(cells, 0, width, axis=dim)
        tail = lax.slice_in_dim(cells, cells.shape[dim] - width, cells.shape[dim], axis=dim)
        cells = jnp.concatenate(
            [
                lax.ppermute(tail, axis, [(i, (i + 1) % count) for i in range(ends)]),
                cells,
                lax.ppermute(head, axis, [((i + 1) % count, i) for i in range(ends)]),
            ],
            axis=dim,
        )
    return cells


def conv_rows(image, weights):
    return lax.conv_general_dilated(
        image,
        weights,
        (1, 1),
        ((0, 0), (1, 1)),
        dimension_numbers=("NCHW", "OIHW", "NCHW"),
        preferred_element_type=jnp.float32,
    )


def dft_tables(width, side, radius):
    freqs = DFT_N // 2 + 1
    f = np.arange(freqs)[None, :]
    x = np.arange(width)[:, None]
    angle = 2 * np.pi * f * x / DFT_N
    forward = np.zeros((width, 2 * LANE))
    forward[:, :freqs] = np.cos(angle)
    forward[:, LANE : LANE + freqs] = -np.sin(angle)
    lag = (np.arange(side) - radius)[:, None]
    tap_angle = 2 * np.pi * f * lag / DFT_N
    taps = np.zeros((side, 2 * LANE))
    taps[:, :freqs] = np.cos(tap_angle)
    taps[:, LANE : LANE + freqs] = np.sin(tap_angle)
    weight = np.full((freqs,), 2.0)
    weight[0] = 1.0
    weight[-1] = 1.0
    back_angle = 2 * np.pi * np.arange(freqs)[:, None] * np.arange(width)[None, :] / DFT_N
    inverse = np.zeros((2 * LANE, width))
    inverse[:freqs] = weight[:, None] * np.cos(back_angle) / DFT_N
    inverse[LANE : LANE + freqs] = -weight[:, None] * np.sin(back_angle) / DFT_N
    return (
        forward.astype(np.float32),
        taps.astype(np.float32),
        inverse.astype(np.float32),
    )


def row_taps_kernel(spec_ref, kern_ref, out_ref):
    group = spec_ref.shape[0]
    side = kern_ref.shape[1]
    rows = out_ref.shape[1]

    def one(c, carry):
        acc_re = jnp.zeros((rows, LANE), jnp.float32)
        acc_im = jnp.zeros((rows, LANE), jnp.float32)
        for u in range(side):
            xr = spec_ref[c, pl.ds(u, rows), pl.ds(0, LANE)]
            xi = spec_ref[c, pl.ds(u, rows), pl.ds(LANE, LANE)]
            kr = kern_ref[c, pl.ds(u, 1), pl.ds(0, LANE)]
            ki = kern_ref[c, pl.ds(u, 1), pl.ds(LANE, LANE)]
            acc_re = acc_re + (kr * xr - ki * xi)
            acc_im = acc_im + (kr * xi + ki * xr)
        out_ref[c, :, pl.ds(0, LANE)] = acc_re
        out_ref[c, :, pl.ds(LANE, LANE)] = acc_im
        return carry

    lax.fori_loop(0, group, one, 0)


def row_taps(spec, kern, rows):
    channels, tall, both = spec.shape
    side = kern.shape[1]
    return pl.pallas_call(
        row_taps_kernel,
        out_shape=jax.ShapeDtypeStruct((channels, rows, both), jnp.float32),
        grid=(channels // GROUP,),
        in_specs=[
            pl.BlockSpec((GROUP, tall, both), lambda g: (g, 0, 0)),
            pl.BlockSpec((GROUP, side, both), lambda g: (g, 0, 0)),
        ],
        out_specs=pl.BlockSpec((GROUP, rows, both), lambda g: (g, 0, 0)),
    )(spec, kern)


def kernel_spectra(psf_bank, psf_index, radius):
    scenes = psf_index.shape[1]
    band_dev = psf_bank.shape[1]
    side = 2 * radius + 1
    unused, taps, unused_too = dft_tables(W, side, radius)
    chosen = psf_bank[psf_index[0, :, 0]].reshape(scenes, band_dev, side, side)
    return jnp.einsum("sbuv,vf->sbuf", chosen, taps, precision=lax.Precision.HIGHEST)


def patch_blur(extended, kern, response, radius):
    band_dev, scenes, tall, width = extended.shape
    rows_dev = tall - 2 * radius
    side = 2 * radius + 1
    forward, unused, inverse = dft_tables(width, side, radius)
    hi = lax.Precision.HIGHEST
    spec = jnp.einsum(
        "cyx,xf->cyf", extended.reshape(band_dev * scenes, tall, width), forward, precision=hi
    )
    taps = kern.transpose(1, 0, 2, 3).reshape(band_dev * scenes, side, -1)
    out = row_taps(spec, taps, rows_dev).reshape(band_dev, scenes, rows_dev, -1)
    color = jnp.einsum("bsyf,bc->scyf", out, response, precision=hi)
    return jnp.einsum("scyf,fx->scyx", color, inverse, precision=hi)


def window_splat(got, band_dev, hit_lanes, scenes):
    slots = got.shape[0]
    energy = got[:, : band_dev * hit_lanes].reshape(slots, band_dev, hit_lanes)
    field = got[:, band_dev * hit_lanes : (band_dev + 1) * hit_lanes].astype(jnp.int32)
    column = got[:, (band_dev + 1) * hit_lanes :].astype(jnp.int32)
    offset = field % WIN
    base = field[:, 0] // WIN
    rows = jnp.arange(WIN, dtype=jnp.int32)
    spread = jnp.where(
        offset[:, None, None, :] == rows[None, None, :, None],
        energy[:, :, None, :],
        jnp.zeros((), energy.dtype),
    )
    onehot = (column[:, :, None] == jnp.arange(W, dtype=jnp.int32)[None, None, :]).astype(
        energy.dtype
    )
    window = jnp.einsum("ibjh,ihc->ibjc", spread, onehot, preferred_element_type=jnp.float32)
    row_ids = jnp.arange(scenes * ROWS_DEV, dtype=jnp.int32)
    placing = (base[:, None, None] + rows[None, :, None] == row_ids[None, None, :]).astype(
        jnp.float32
    )
    total = jnp.einsum("ibjc,ijr->brc", window, placing, precision=lax.Precision.HIGH)
    return total.reshape(band_dev, scenes, ROWS_DEV, W)


def pack_kernel(capacity, energy_ref, spot_ref, tile_ref, count_ref, scene_ref, row_ref, out_ref):
    blocks, bands, hits = energy_ref.shape
    width = bands * hits
    slots = out_ref.shape[0]
    tiles = slots // capacity
    f32 = jnp.float32
    ii = lax.broadcasted_iota(jnp.int32, (blocks, blocks), 0)
    jj = lax.broadcasted_iota(jnp.int32, (blocks, blocks), 1)
    eye = ii == jj
    tile_row = tile_ref[...].astype(f32)
    count_row = count_ref[...].astype(f32)
    base_row = (scene_ref[...] * ROWS_DEV + row_ref[...]).astype(f32)
    zero = jnp.zeros((blocks, blocks), f32)
    count_col = jnp.sum(jnp.where(eye, count_row, zero), axis=1, keepdims=True)
    base_col = jnp.sum(jnp.where(eye, base_row, zero), axis=1, keepdims=True)
    lanes = lax.broadcasted_iota(jnp.int32, (blocks, hits), 1)
    live = lanes.astype(f32) < count_col
    spot = spot_ref[...]
    field = base_col * WIN + lax.shift_right_logical(spot, 7).astype(f32)
    column = jnp.bitwise_and(spot, W - 1).astype(f32)
    tt = lax.broadcasted_iota(jnp.int32, (tiles, blocks), 0).astype(f32)
    owners = (tt == tile_row).astype(jnp.bfloat16)
    earlier = (ii < jj).astype(jnp.bfloat16)
    before = jnp.dot(owners, earlier, preferred_element_type=f32)
    rank = jnp.sum(before * owners.astype(f32), axis=0, keepdims=True)
    place = tile_row * capacity + rank
    pp = lax.broadcasted_iota(jnp.int32, (slots, blocks), 0).astype(f32)
    select = (pp == place).astype(jnp.bfloat16)
    for band in range(bands):
        energy = energy_ref[:, band, :]
        masked = jnp.where(live, energy, jnp.zeros_like(energy))
        out_ref[:, pl.ds(band * hits, hits)] = jnp.dot(
            select, masked, preferred_element_type=f32
        ).astype(out_ref.dtype)
    out_ref[:, pl.ds(width, hits)] = jnp.dot(
        select, field.astype(jnp.bfloat16), preferred_element_type=f32
    ).astype(out_ref.dtype)
    out_ref[:, pl.ds(width + hits, hits)] = jnp.dot(
        select, column.astype(jnp.bfloat16), preferred_element_type=f32
    ).astype(out_ref.dtype)


def pack(energy, spot, tile, count, scene, row, capacity, slots):
    blocks, bands, hits = energy.shape
    width = bands * hits
    return pl.pallas_call(
        functools.partial(pack_kernel, capacity),
        out_shape=jax.ShapeDtypeStruct((slots, width + 2 * hits), energy.dtype),
    )(energy, spot, tile, count, scene, row)


def per_device(
    hit_energy,
    hit_spot,
    block_tile,
    block_count,
    block_scene,
    block_row,
    psf_bank,
    psf_index,
    response,
    conv_in,
    conv_out,
):
    tile_count = lax.axis_size("tile")
    wave_count = lax.axis_size("wave")
    block_dev, band_dev, hit_lanes = hit_energy.shape
    capacity = 2 * block_dev // tile_count
    scenes = psf_index.shape[1]
    send = pack(
        hit_energy,
        hit_spot[0],
        block_tile[0, :, 0].reshape(1, block_dev),
        block_count,
        block_scene,
        block_row,
        capacity,
        tile_count * capacity,
    )
    kern = kernel_spectra(psf_bank, psf_index, K // 2)
    got = lax.all_to_all(send, "tile", split_axis=0, concat_axis=0, tiled=True)
    splat = window_splat(got, band_dev, hit_lanes, scenes)
    extended = padded_2(splat, (("tile", 2),), K // 2)
    wave_index = lax.axis_index("wave")
    my_response = lax.dynamic_slice_in_dim(response, wave_index * band_dev, band_dev, 0)
    partial = patch_blur(extended, kern, my_response, K // 2)
    color = lax.dynamic_index_in_dim(partial, wave_index, 0, keepdims=False)
    for step in range(1, wave_count):
        piece = lax.dynamic_index_in_dim(partial, (wave_index + step) % wave_count, 0, keepdims=False)
        color = color + lax.ppermute(
            piece, "wave", [(i, (i + step) % wave_count) for i in range(wave_count)]
        )
    sensor = lax.reduce_precision(color[None], exponent_bits=8, mantissa_bits=7)
    sensor = sensor.astype(jnp.bfloat16)
    rimmed = padded_2(sensor, (("tile", 2),), 2)
    hidden = jax.nn.silu(conv_rows(rimmed, conv_in))
    hidden = lax.reduce_precision(hidden, exponent_bits=8, mantissa_bits=7).astype(jnp.bfloat16)
    tile_index = lax.axis_index("tile")
    row_ids = lax.broadcasted_iota(jnp.int32, hidden.shape, 2)
    outside = ((tile_index == 0) & (row_ids == 0)) | (
        (tile_index == tile_count - 1) & (row_ids == hidden.shape[2] - 1)
    )
    hidden = jnp.where(outside, jnp.zeros_like(hidden), hidden)
    return conv_rows(hidden, conv_out).astype(jnp.bfloat16)


def solution(mesh):
    in_specs = (
        P("tile", "wave", None),
        P("wave", "tile", None),
        P("wave", "tile", None),
        P("wave", "tile"),
        P("wave", "tile"),
        P("wave", "tile"),
        P(None, "wave", None),
        P("tile", None, None),
        P(),
        P(),
        P(),
    )
    out_specs = P("wave", None, "tile", None)
    return jax.shard_map(
        per_device, mesh=mesh, in_specs=in_specs, out_specs=out_specs, check_vma=False
    )
```

```python
import functools

import jax
import jax.numpy as jnp
import numpy as np
from jax import lax
from jax.experimental import pallas as pl
from jax.sharding import PartitionSpec as P

ROWS_DEV = 16
W = 128
WIN = 4
K = 31
DFT_N = 144
LANE = 128
GROUP = 8


def padded_2(cells, sides, width):
    for axis, dim in sides:
        count = lax.axis_size(axis)
        ends = count - 1
        head = lax.slice_in_dim(cells, 0, width, axis=dim)
        tail = lax.slice_in_dim(cells, cells.shape[dim] - width, cells.shape[dim], axis=dim)
        cells = jnp.concatenate(
            [
                lax.ppermute(tail, axis, [(i, (i + 1) % count) for i in range(ends)]),
                cells,
                lax.ppermute(head, axis, [((i + 1) % count, i) for i in range(ends)]),
            ],
            axis=dim,
        )
    return cells


def conv_rows(image, weights):
    return lax.conv_general_dilated(
        image,
        weights,
        (1, 1),
        ((0, 0), (1, 1)),
        dimension_numbers=("NCHW", "OIHW", "NCHW"),
        preferred_element_type=jnp.float32,
    )


def dft_tables(width, side, radius):
    freqs = DFT_N // 2 + 1
    f = np.arange(freqs)[None, :]
    x = np.arange(width)[:, None]
    angle = 2 * np.pi * f * x / DFT_N
    forward = np.zeros((width, 2 * LANE))
    forward[:, :freqs] = np.cos(angle)
    forward[:, LANE : LANE + freqs] = -np.sin(angle)
    lag = (np.arange(side) - radius)[:, None]
    tap_angle = 2 * np.pi * f * lag / DFT_N
    taps = np.zeros((side, 2 * LANE))
    taps[:, :freqs] = np.cos(tap_angle)
    taps[:, LANE : LANE + freqs] = np.sin(tap_angle)
    weight = np.full((freqs,), 2.0)
    weight[0] = 1.0
    weight[-1] = 1.0
    back_angle = 2 * np.pi * np.arange(freqs)[:, None] * np.arange(width)[None, :] / DFT_N
    inverse = np.zeros((2 * LANE, width))
    inverse[:freqs] = weight[:, None] * np.cos(back_angle) / DFT_N
    inverse[LANE : LANE + freqs] = -weight[:, None] * np.sin(back_angle) / DFT_N
    return (
        forward.astype(np.float32),
        taps.astype(np.float32),
        inverse.astype(np.float32),
    )


def row_taps_kernel(spec_ref, kern_ref, out_ref):
    group, tall = spec_ref.shape[:2]
    rows = out_ref.shape[1]
    side = tall - rows + 1

    def one(c, carry):
        acc_re = jnp.zeros((rows, LANE), jnp.float32)
        acc_im = jnp.zeros((rows, LANE), jnp.float32)
        for u in range(side):
            xr = spec_ref[c, pl.ds(u, rows), pl.ds(0, LANE)]
            xi = spec_ref[c, pl.ds(u, rows), pl.ds(LANE, LANE)]
            kr = kern_ref[c, pl.ds(u, 1), pl.ds(0, LANE)]
            ki = kern_ref[c, pl.ds(u, 1), pl.ds(LANE, LANE)]
            acc_re = acc_re + (kr * xr - ki * xi)
            acc_im = acc_im + (kr * xi + ki * xr)
        out_ref[c, :, pl.ds(0, LANE)] = acc_re
        out_ref[c, :, pl.ds(LANE, LANE)] = acc_im
        return carry

    lax.fori_loop(0, group, one, 0)


def row_taps(spec, kern, rows):
    channels, tall, both = spec.shape
    side = kern.shape[1]
    return pl.pallas_call(
        row_taps_kernel,
        out_shape=jax.ShapeDtypeStruct((channels, rows, both), jnp.float32),
        grid=(channels // GROUP,),
        in_specs=[
            pl.BlockSpec((GROUP, tall, both), lambda g: (g, 0, 0)),
            pl.BlockSpec((GROUP, side, both), lambda g: (g, 0, 0)),
        ],
        out_specs=pl.BlockSpec((GROUP, rows, both), lambda g: (g, 0, 0)),
    )(spec, kern)


def kernel_spectra(psf_bank, psf_index, radius):
    scenes = psf_index.shape[1]
    band_dev = psf_bank.shape[1]
    side = 2 * radius + 1
    unused, taps, unused_too = dft_tables(W, side, radius)
    chosen = psf_bank[psf_index[0, :, 0]].reshape(scenes, band_dev, side, side)
    chosen = jnp.pad(chosen.transpose(1, 0, 2, 3), ((0, 0), (0, 0), (0, 1), (0, 0)))
    spectra = jnp.dot(
        chosen.reshape(-1, side), taps, precision=lax.Precision.HIGHEST
    )
    return spectra.reshape(band_dev * scenes, side + 1, -1)


def patch_blur(extended, kern, response, radius):
    band_dev, scenes, tall, width = extended.shape
    rows_dev = tall - 2 * radius
    side = 2 * radius + 1
    forward, unused, inverse = dft_tables(width, side, radius)
    hi = lax.Precision.HIGHEST
    spec = jnp.einsum(
        "cyx,xf->cyf", extended.reshape(band_dev * scenes, tall, width), forward, precision=hi
    )
    taps = kern
    out = row_taps(spec, taps, rows_dev).reshape(band_dev, scenes, rows_dev, -1)
    color = jnp.einsum("bsyf,bc->scyf", out, response, precision=hi)
    return jnp.einsum("scyf,fx->scyx", color, inverse, precision=hi)


def window_splat(got, band_dev, hit_lanes, scenes):
    slots = got.shape[0]
    energy = got[:, : band_dev * hit_lanes].reshape(slots, band_dev, hit_lanes)
    field = got[:, band_dev * hit_lanes : (band_dev + 1) * hit_lanes].astype(jnp.int32)
    column = got[:, (band_dev + 1) * hit_lanes :].astype(jnp.int32)
    offset = field % WIN
    base = field[:, 0] // WIN
    rows = jnp.arange(WIN, dtype=jnp.int32)
    spread = jnp.where(
        offset[:, None, None, :] == rows[None, None, :, None],
        energy[:, :, None, :],
        jnp.zeros((), energy.dtype),
    )
    onehot = (column[:, :, None] == jnp.arange(W, dtype=jnp.int32)[None, None, :]).astype(
        energy.dtype
    )
    window = jnp.einsum("ibjh,ihc->ibjc", spread, onehot, preferred_element_type=jnp.float32)
    row_ids = jnp.arange(scenes * ROWS_DEV, dtype=jnp.int32)
    placing = (base[:, None, None] + rows[None, :, None] == row_ids[None, None, :]).astype(
        jnp.float32
    )
    placing = placing.astype(jnp.bfloat16)
    upper = lax.reduce_precision(window, exponent_bits=8, mantissa_bits=7)
    lower = (window - upper).astype(jnp.bfloat16)
    total = jnp.einsum(
        "ibjc,ijr->brc", upper.astype(jnp.bfloat16), placing, preferred_element_type=jnp.float32
    ) + jnp.einsum("ibjc,ijr->brc", lower, placing, preferred_element_type=jnp.float32)
    return total.reshape(band_dev, scenes, ROWS_DEV, W)


def pack_kernel(capacity, energy_ref, spot_ref, tile_ref, count_ref, scene_ref, row_ref, out_ref):
    blocks, bands, hits = energy_ref.shape
    width = bands * hits
    slots = out_ref.shape[0]
    tiles = slots // capacity
    f32 = jnp.float32
    ii = lax.broadcasted_iota(jnp.int32, (blocks, blocks), 0)
    jj = lax.broadcasted_iota(jnp.int32, (blocks, blocks), 1)
    eye = ii == jj
    tile_row = tile_ref[...].astype(f32)
    count_row = count_ref[...].astype(f32)
    base_row = (scene_ref[...] * ROWS_DEV + row_ref[...]).astype(f32)
    zero = jnp.zeros((blocks, blocks), f32)
    count_col = jnp.sum(jnp.where(eye, count_row, zero), axis=1, keepdims=True)
    base_col = jnp.sum(jnp.where(eye, base_row, zero), axis=1, keepdims=True)
    lanes = lax.broadcasted_iota(jnp.int32, (blocks, hits), 1)
    live = lanes.astype(f32) < count_col
    spot = spot_ref[...]
    field = base_col * WIN + lax.shift_right_logical(spot, 7).astype(f32)
    column = jnp.bitwise_and(spot, W - 1).astype(f32)
    tt = lax.broadcasted_iota(jnp.int32, (tiles, blocks), 0).astype(f32)
    owners = (tt == tile_row).astype(jnp.bfloat16)
    earlier = (ii < jj).astype(jnp.bfloat16)
    before = jnp.dot(owners, earlier, preferred_element_type=f32)
    rank = jnp.sum(before * owners.astype(f32), axis=0, keepdims=True)
    place = tile_row * capacity + rank
    pp = lax.broadcasted_iota(jnp.int32, (slots, blocks), 0).astype(f32)
    select = (pp == place).astype(jnp.bfloat16)
    for band in range(bands):
        energy = energy_ref[:, band, :]
        masked = jnp.where(live, energy, jnp.zeros_like(energy))
        out_ref[:, pl.ds(band * hits, hits)] = jnp.dot(
            select, masked, preferred_element_type=f32
        ).astype(out_ref.dtype)
    out_ref[:, pl.ds(width, hits)] = jnp.dot(
        select, field.astype(jnp.bfloat16), preferred_element_type=f32
    ).astype(out_ref.dtype)
    out_ref[:, pl.ds(width + hits, hits)] = jnp.dot(
        select, column.astype(jnp.bfloat16), preferred_element_type=f32
    ).astype(out_ref.dtype)


def pack(energy, spot, tile, count, scene, row, capacity, slots):
    blocks, bands, hits = energy.shape
    width = bands * hits
    return pl.pallas_call(
        functools.partial(pack_kernel, capacity),
        out_shape=jax.ShapeDtypeStruct((slots, width + 2 * hits), energy.dtype),
    )(energy, spot, tile, count, scene, row)


def per_device(
    hit_energy,
    hit_spot,
    block_tile,
    block_count,
    block_scene,
    block_row,
    psf_bank,
    psf_index,
    response,
    conv_in,
    conv_out,
):
    tile_count = lax.axis_size("tile")
    wave_count = lax.axis_size("wave")
    block_dev, band_dev, hit_lanes = hit_energy.shape
    capacity = 2 * block_dev // tile_count
    scenes = psf_index.shape[1]
    send = pack(
        hit_energy,
        hit_spot[0],
        block_tile[0, :, 0].reshape(1, block_dev),
        block_count,
        block_scene,
        block_row,
        capacity,
        tile_count * capacity,
    )
    kern = kernel_spectra(psf_bank, psf_index, K // 2)
    got = lax.all_to_all(send, "tile", split_axis=0, concat_axis=0, tiled=True)
    splat = window_splat(got, band_dev, hit_lanes, scenes)
    extended = padded_2(splat, (("tile", 2),), K // 2)
    wave_index = lax.axis_index("wave")
    my_response = lax.dynamic_slice_in_dim(response, wave_index * band_dev, band_dev, 0)
    partial = patch_blur(extended, kern, my_response, K // 2)
    color = lax.dynamic_index_in_dim(partial, wave_index, 0, keepdims=False)
    for step in range(1, wave_count):
        piece = lax.dynamic_index_in_dim(partial, (wave_index + step) % wave_count, 0, keepdims=False)
        color = color + lax.ppermute(
            piece, "wave", [(i, (i + step) % wave_count) for i in range(wave_count)]
        )
    sensor = lax.reduce_precision(color[None], exponent_bits=8, mantissa_bits=7)
    sensor = sensor.astype(jnp.bfloat16)
    rimmed = padded_2(sensor, (("tile", 2),), 2)
    hidden = jax.nn.silu(conv_rows(rimmed, conv_in))
    hidden = lax.reduce_precision(hidden, exponent_bits=8, mantissa_bits=7).astype(jnp.bfloat16)
    tile_index = lax.axis_index("tile")
    row_ids = lax.broadcasted_iota(jnp.int32, hidden.shape, 2)
    outside = ((tile_index == 0) & (row_ids == 0)) | (
        (tile_index == tile_count - 1) & (row_ids == hidden.shape[2] - 1)
    )
    hidden = jnp.where(outside, jnp.zeros_like(hidden), hidden)
    return conv_rows(hidden, conv_out).astype(jnp.bfloat16)


def solution(mesh):
    in_specs = (
        P("tile", "wave", None),
        P("wave", "tile", None),
        P("wave", "tile", None),
        P("wave", "tile"),
        P("wave", "tile"),
        P("wave", "tile"),
        P(None, "wave", None),
        P("tile", None, None),
        P(),
        P(),
        P(),
    )
    out_specs = P("wave", None, "tile", None)
    return jax.shard_map(
        per_device, mesh=mesh, in_specs=in_specs, out_specs=out_specs, check_vma=False
    )
```

```python
import functools

import jax
import jax.numpy as jnp
import numpy as np
from jax import lax
from jax.experimental import pallas as pl
from jax.sharding import PartitionSpec as P

ROWS_DEV = 16
W = 128
WIN = 4
K = 31
DFT_N = 144
LANE = 128
GROUP = 8


def padded_2(cells, sides, width):
    for axis, dim in sides:
        count = lax.axis_size(axis)
        ends = count - 1
        head = lax.slice_in_dim(cells, 0, width, axis=dim)
        tail = lax.slice_in_dim(cells, cells.shape[dim] - width, cells.shape[dim], axis=dim)
        cells = jnp.concatenate(
            [
                lax.ppermute(tail, axis, [(i, (i + 1) % count) for i in range(ends)]),
                cells,
                lax.ppermute(head, axis, [((i + 1) % count, i) for i in range(ends)]),
            ],
            axis=dim,
        )
    return cells


def conv_rows(image, weights):
    return lax.conv_general_dilated(
        image,
        weights,
        (1, 1),
        ((0, 0), (1, 1)),
        dimension_numbers=("NCHW", "OIHW", "NCHW"),
        preferred_element_type=jnp.float32,
    )


def dft_tables(width, side, radius):
    freqs = DFT_N // 2 + 1
    f = np.arange(freqs)[None, :]
    x = np.arange(width)[:, None]
    angle = 2 * np.pi * f * x / DFT_N
    forward = np.zeros((width, 2 * LANE))
    forward[:, :freqs] = np.cos(angle)
    forward[:, LANE : LANE + freqs] = -np.sin(angle)
    lag = (np.arange(side) - radius)[:, None]
    tap_angle = 2 * np.pi * f * lag / DFT_N
    taps = np.zeros((side, 2 * LANE))
    taps[:, :freqs] = np.cos(tap_angle)
    taps[:, LANE : LANE + freqs] = np.sin(tap_angle)
    weight = np.full((freqs,), 2.0)
    weight[0] = 1.0
    weight[-1] = 1.0
    back_angle = 2 * np.pi * np.arange(freqs)[:, None] * np.arange(width)[None, :] / DFT_N
    inverse = np.zeros((2 * LANE, width))
    inverse[:freqs] = weight[:, None] * np.cos(back_angle) / DFT_N
    inverse[LANE : LANE + freqs] = -weight[:, None] * np.sin(back_angle) / DFT_N
    return (
        forward.astype(np.float32),
        taps.astype(np.float32),
        inverse.astype(np.float32),
    )


def row_taps_kernel(spec_ref, kern_ref, out_ref):
    group, tall = spec_ref.shape[:2]
    rows = out_ref.shape[1]
    side = tall - rows + 1

    def one(c, carry):
        acc_re = jnp.zeros((rows, LANE), jnp.float32)
        acc_im = jnp.zeros((rows, LANE), jnp.float32)
        for u in range(side):
            xr = spec_ref[c, pl.ds(u, rows), pl.ds(0, LANE)]
            xi = spec_ref[c, pl.ds(u, rows), pl.ds(LANE, LANE)]
            kr = kern_ref[c, pl.ds(u, 1), pl.ds(0, LANE)]
            ki = kern_ref[c, pl.ds(u, 1), pl.ds(LANE, LANE)]
            acc_re = acc_re + (kr * xr - ki * xi)
            acc_im = acc_im + (kr * xi + ki * xr)
        out_ref[c, :, pl.ds(0, LANE)] = acc_re
        out_ref[c, :, pl.ds(LANE, LANE)] = acc_im
        return carry

    lax.fori_loop(0, group, one, 0)


def row_taps(spec, kern, rows):
    channels, tall, both = spec.shape
    side = kern.shape[1]
    return pl.pallas_call(
        row_taps_kernel,
        out_shape=jax.ShapeDtypeStruct((channels, rows, both), jnp.float32),
        grid=(channels // GROUP,),
        in_specs=[
            pl.BlockSpec((GROUP, tall, both), lambda g: (g, 0, 0)),
            pl.BlockSpec((GROUP, side, both), lambda g: (g, 0, 0)),
        ],
        out_specs=pl.BlockSpec((GROUP, rows, both), lambda g: (g, 0, 0)),
    )(spec, kern)


def kernel_spectra(psf_bank, psf_index, radius):
    scenes = psf_index.shape[1]
    band_dev = psf_bank.shape[1]
    side = 2 * radius + 1
    unused, taps, unused_too = dft_tables(W, side, radius)
    chosen = psf_bank[psf_index[0, :, 0]].reshape(scenes, band_dev, side, side)
    chosen = jnp.pad(chosen.transpose(1, 0, 2, 3), ((0, 0), (0, 0), (0, 1), (0, 0)))
    spectra = jnp.dot(
        chosen.reshape(-1, side), taps, precision=lax.Precision.HIGHEST
    )
    return spectra.reshape(band_dev * scenes, side + 1, -1)


def patch_blur(extended, kern, response, radius):
    band_dev, scenes, tall, width = extended.shape
    rows_dev = tall - 2 * radius
    side = 2 * radius + 1
    forward, unused, inverse = dft_tables(width, side, radius)
    hi = lax.Precision.HIGHEST
    spec = jnp.einsum(
        "cyx,xf->cyf", extended.reshape(band_dev * scenes, tall, width), forward, precision=hi
    )
    taps = kern
    out = row_taps(spec, taps, rows_dev).reshape(band_dev, scenes, rows_dev, -1)
    color = jnp.einsum("bsyf,bc->scyf", out, response, precision=hi)
    return jnp.einsum("scyf,fx->scyx", color, inverse, precision=hi)


def window_splat(got, band_dev, hit_lanes, scenes):
    slots = got.shape[0]
    energy = got[:, : band_dev * hit_lanes].reshape(slots, band_dev, hit_lanes)
    field = got[:, band_dev * hit_lanes : (band_dev + 1) * hit_lanes].astype(jnp.int32)
    column = got[:, (band_dev + 1) * hit_lanes :].astype(jnp.int32)
    offset = field % WIN
    base = field[:, 0] // WIN
    rows = jnp.arange(WIN, dtype=jnp.int32)
    spread = jnp.where(
        offset[:, None, None, :] == rows[None, None, :, None],
        energy[:, :, None, :],
        jnp.zeros((), energy.dtype),
    )
    onehot = (column[:, :, None] == jnp.arange(W, dtype=jnp.int32)[None, None, :]).astype(
        energy.dtype
    )
    window = jnp.einsum("ibjh,ihc->ibjc", spread, onehot, preferred_element_type=jnp.float32)
    row_ids = jnp.arange(scenes * ROWS_DEV, dtype=jnp.int32)
    placing = (base[:, None, None] + rows[None, :, None] == row_ids[None, None, :]).astype(
        jnp.float32
    )
    placing = placing.astype(jnp.bfloat16)
    upper = lax.reduce_precision(window, exponent_bits=8, mantissa_bits=7)
    lower = (window - upper).astype(jnp.bfloat16)
    total = jnp.einsum(
        "ibjc,ijr->brc", upper.astype(jnp.bfloat16), placing, preferred_element_type=jnp.float32
    ) + jnp.einsum("ibjc,ijr->brc", lower, placing, preferred_element_type=jnp.float32)
    return total.reshape(band_dev, scenes, ROWS_DEV, W)


def pack_kernel(capacity, energy_ref, spot_ref, tile_ref, count_ref, scene_ref, row_ref, out_ref):
    blocks, bands, hits = energy_ref.shape
    width = bands * hits
    slots = out_ref.shape[0]
    tiles = slots // capacity
    f32 = jnp.float32
    ii = lax.broadcasted_iota(jnp.int32, (blocks, blocks), 0)
    jj = lax.broadcasted_iota(jnp.int32, (blocks, blocks), 1)
    eye = ii == jj
    tile_row = tile_ref[...].astype(f32)
    count_row = count_ref[...].astype(f32)
    base_row = (scene_ref[...] * ROWS_DEV + row_ref[...]).astype(f32)
    zero = jnp.zeros((blocks, blocks), f32)
    count_col = jnp.sum(jnp.where(eye, count_row, zero), axis=1, keepdims=True)
    base_col = jnp.sum(jnp.where(eye, base_row, zero), axis=1, keepdims=True)
    lanes = lax.broadcasted_iota(jnp.int32, (blocks, hits), 1)
    live = lanes.astype(f32) < count_col
    spot = spot_ref[...]
    field = base_col * WIN + lax.shift_right_logical(spot, 7).astype(f32)
    column = jnp.bitwise_and(spot, W - 1).astype(f32)
    tt = lax.broadcasted_iota(jnp.int32, (tiles, blocks), 0).astype(f32)
    owners = (tt == tile_row).astype(jnp.bfloat16)
    earlier = (ii < jj).astype(jnp.bfloat16)
    before = jnp.dot(owners, earlier, preferred_element_type=f32)
    rank = jnp.sum(before * owners.astype(f32), axis=0, keepdims=True)
    place = tile_row * capacity + rank
    pp = lax.broadcasted_iota(jnp.int32, (slots, blocks), 0).astype(f32)
    select = (pp == place).astype(jnp.bfloat16)
    for band in range(bands):
        energy = energy_ref[:, band, :]
        masked = jnp.where(live, energy, jnp.zeros_like(energy))
        out_ref[:, pl.ds(band * hits, hits)] = jnp.dot(
            select, masked, preferred_element_type=f32
        ).astype(out_ref.dtype)
    out_ref[:, pl.ds(width, hits)] = jnp.dot(
        select, field.astype(jnp.bfloat16), preferred_element_type=f32
    ).astype(out_ref.dtype)
    out_ref[:, pl.ds(width + hits, hits)] = jnp.dot(
        select, column.astype(jnp.bfloat16), preferred_element_type=f32
    ).astype(out_ref.dtype)


def pack(energy, spot, tile, count, scene, row, capacity, slots):
    blocks, bands, hits = energy.shape
    width = bands * hits
    return pl.pallas_call(
        functools.partial(pack_kernel, capacity),
        out_shape=jax.ShapeDtypeStruct((slots, width + 2 * hits), energy.dtype),
    )(energy, spot, tile, count, scene, row)


def per_device(
    hit_energy,
    hit_spot,
    block_tile,
    block_count,
    block_scene,
    block_row,
    psf_bank,
    psf_index,
    response,
    conv_in,
    conv_out,
):
    tile_count = lax.axis_size("tile")
    wave_count = lax.axis_size("wave")
    block_dev, band_dev, hit_lanes = hit_energy.shape
    capacity = 2 * block_dev // tile_count
    scenes = psf_index.shape[1]
    send = pack(
        hit_energy,
        hit_spot[0],
        block_tile[0, :, 0].reshape(1, block_dev),
        block_count,
        block_scene,
        block_row,
        capacity,
        tile_count * capacity,
    )
    kern = kernel_spectra(psf_bank, psf_index, K // 2)
    got = lax.all_to_all(send, "tile", split_axis=0, concat_axis=0, tiled=True)
    got, kern = lax.optimization_barrier((got, kern))
    splat = window_splat(got, band_dev, hit_lanes, scenes)
    extended = padded_2(splat, (("tile", 2),), K // 2)
    wave_index = lax.axis_index("wave")
    my_response = lax.dynamic_slice_in_dim(response, wave_index * band_dev, band_dev, 0)
    partial = patch_blur(extended, kern, my_response, K // 2)
    color = lax.dynamic_index_in_dim(partial, wave_index, 0, keepdims=False)
    for step in range(1, wave_count):
        piece = lax.dynamic_index_in_dim(partial, (wave_index + step) % wave_count, 0, keepdims=False)
        color = color + lax.ppermute(
            piece, "wave", [(i, (i + step) % wave_count) for i in range(wave_count)]
        )
    sensor = lax.reduce_precision(color[None], exponent_bits=8, mantissa_bits=7)
    sensor = sensor.astype(jnp.bfloat16)
    rimmed = padded_2(sensor, (("tile", 2),), 2)
    hidden = jax.nn.silu(conv_rows(rimmed, conv_in))
    hidden = lax.reduce_precision(hidden, exponent_bits=8, mantissa_bits=7).astype(jnp.bfloat16)
    tile_index = lax.axis_index("tile")
    row_ids = lax.broadcasted_iota(jnp.int32, hidden.shape, 2)
    outside = ((tile_index == 0) & (row_ids == 0)) | (
        (tile_index == tile_count - 1) & (row_ids == hidden.shape[2] - 1)
    )
    hidden = jnp.where(outside, jnp.zeros_like(hidden), hidden)
    return conv_rows(hidden, conv_out).astype(jnp.bfloat16)


def solution(mesh):
    in_specs = (
        P("tile", "wave", None),
        P("wave", "tile", None),
        P("wave", "tile", None),
        P("wave", "tile"),
        P("wave", "tile"),
        P("wave", "tile"),
        P(None, "wave", None),
        P("tile", None, None),
        P(),
        P(),
        P(),
    )
    out_specs = P("wave", None, "tile", None)
    return jax.shard_map(
        per_device, mesh=mesh, in_specs=in_specs, out_specs=out_specs, check_vma=False
    )
```

```python
import functools

import jax
import jax.numpy as jnp
import numpy as np
from jax import lax
from jax.experimental import pallas as pl
from jax.sharding import PartitionSpec as P

ROWS_DEV = 16
W = 128
WIN = 4
K = 31
DFT_N = 144
LANE = 128
GROUP = 8


def padded_2(cells, sides, width):
    for axis, dim in sides:
        count = lax.axis_size(axis)
        ends = count - 1
        head = lax.slice_in_dim(cells, 0, width, axis=dim)
        tail = lax.slice_in_dim(cells, cells.shape[dim] - width, cells.shape[dim], axis=dim)
        cells = jnp.concatenate(
            [
                lax.ppermute(tail, axis, [(i, (i + 1) % count) for i in range(ends)]),
                cells,
                lax.ppermute(head, axis, [((i + 1) % count, i) for i in range(ends)]),
            ],
            axis=dim,
        )
    return cells


def conv_rows(image, weights):
    return lax.conv_general_dilated(
        image,
        weights,
        (1, 1),
        ((0, 0), (1, 1)),
        dimension_numbers=("NCHW", "OIHW", "NCHW"),
        preferred_element_type=jnp.float32,
    )


def dft_tables(width, side, radius):
    freqs = DFT_N // 2 + 1
    f = np.arange(freqs)[None, :]
    x = np.arange(width)[:, None]
    angle = 2 * np.pi * f * x / DFT_N
    forward = np.zeros((width, 2 * LANE))
    forward[:, :freqs] = np.cos(angle)
    forward[:, LANE : LANE + freqs] = -np.sin(angle)
    lag = (np.arange(side) - radius)[:, None]
    tap_angle = 2 * np.pi * f * lag / DFT_N
    taps = np.zeros((side, 2 * LANE))
    taps[:, :freqs] = np.cos(tap_angle)
    taps[:, LANE : LANE + freqs] = np.sin(tap_angle)
    weight = np.full((freqs,), 2.0)
    weight[0] = 1.0
    weight[-1] = 1.0
    back_angle = 2 * np.pi * np.arange(freqs)[:, None] * np.arange(width)[None, :] / DFT_N
    inverse = np.zeros((2 * LANE, width))
    inverse[:freqs] = weight[:, None] * np.cos(back_angle) / DFT_N
    inverse[LANE : LANE + freqs] = -weight[:, None] * np.sin(back_angle) / DFT_N
    return (
        forward.astype(np.float32),
        taps.astype(np.float32),
        inverse.astype(np.float32),
    )


def row_taps_kernel(spec_ref, kern_ref, out_ref):
    group, tall = spec_ref.shape[:2]
    rows = out_ref.shape[1]
    side = tall - rows + 1

    def one(c, carry):
        acc_re = jnp.zeros((rows, LANE), jnp.float32)
        acc_im = jnp.zeros((rows, LANE), jnp.float32)
        for u in range(side):
            xr = spec_ref[c, pl.ds(u, rows), pl.ds(0, LANE)]
            xi = spec_ref[c, pl.ds(u, rows), pl.ds(LANE, LANE)]
            kr = kern_ref[c, pl.ds(u, 1), pl.ds(0, LANE)]
            ki = kern_ref[c, pl.ds(u, 1), pl.ds(LANE, LANE)]
            acc_re = acc_re + (kr * xr - ki * xi)
            acc_im = acc_im + (kr * xi + ki * xr)
        out_ref[c, :, pl.ds(0, LANE)] = acc_re
        out_ref[c, :, pl.ds(LANE, LANE)] = acc_im
        return carry

    lax.fori_loop(0, group, one, 0)


def row_taps(spec, kern, rows):
    channels, tall, both = spec.shape
    side = kern.shape[1]
    return pl.pallas_call(
        row_taps_kernel,
        out_shape=jax.ShapeDtypeStruct((channels, rows, both), jnp.float32),
        grid=(channels // GROUP,),
        in_specs=[
            pl.BlockSpec((GROUP, tall, both), lambda g: (g, 0, 0)),
            pl.BlockSpec((GROUP, side, both), lambda g: (g, 0, 0)),
        ],
        out_specs=pl.BlockSpec((GROUP, rows, both), lambda g: (g, 0, 0)),
    )(spec, kern)


def kernel_spectra(psf_bank, psf_index, radius):
    scenes = psf_index.shape[1]
    band_dev = psf_bank.shape[1]
    side = 2 * radius + 1
    unused, taps, unused_too = dft_tables(W, side, radius)
    chosen = psf_bank[psf_index[0, :, 0]].reshape(scenes, band_dev, side, side)
    chosen = jnp.pad(chosen.transpose(1, 0, 2, 3), ((0, 0), (0, 0), (0, 1), (0, 0)))
    spectra = jnp.dot(
        chosen.reshape(-1, side), taps, precision=lax.Precision.HIGHEST
    )
    return spectra.reshape(band_dev * scenes, side + 1, -1)


def patch_blur(extended, kern, response, radius):
    band_dev, scenes, tall, width = extended.shape
    rows_dev = tall - 2 * radius
    side = 2 * radius + 1
    forward, unused, inverse = dft_tables(width, side, radius)
    hi = lax.Precision.HIGH
    spec = jnp.einsum(
        "cyx,xf->cyf", extended.reshape(band_dev * scenes, tall, width), forward, precision=hi
    )
    taps = kern
    out = row_taps(spec, taps, rows_dev).reshape(band_dev, scenes, rows_dev, -1)
    color = jnp.einsum("bsyf,bc->scyf", out, response, precision=hi)
    return jnp.einsum("scyf,fx->scyx", color, inverse, precision=hi)


def window_splat(got, band_dev, hit_lanes, scenes):
    slots = got.shape[0]
    energy = got[:, : band_dev * hit_lanes].reshape(slots, band_dev, hit_lanes)
    field = got[:, band_dev * hit_lanes : (band_dev + 1) * hit_lanes].astype(jnp.int32)
    column = got[:, (band_dev + 1) * hit_lanes :].astype(jnp.int32)
    offset = field % WIN
    base = field[:, 0] // WIN
    rows = jnp.arange(WIN, dtype=jnp.int32)
    spread = jnp.where(
        offset[:, None, None, :] == rows[None, None, :, None],
        energy[:, :, None, :],
        jnp.zeros((), energy.dtype),
    )
    onehot = (column[:, :, None] == jnp.arange(W, dtype=jnp.int32)[None, None, :]).astype(
        energy.dtype
    )
    window = jnp.einsum("ibjh,ihc->ibjc", spread, onehot, preferred_element_type=jnp.float32)
    row_ids = jnp.arange(scenes * ROWS_DEV, dtype=jnp.int32)
    placing = (base[:, None, None] + rows[None, :, None] == row_ids[None, None, :]).astype(
        jnp.float32
    )
    placing = placing.astype(jnp.bfloat16)
    upper = lax.reduce_precision(window, exponent_bits=8, mantissa_bits=7)
    lower = (window - upper).astype(jnp.bfloat16)
    total = jnp.einsum(
        "ibjc,ijr->brc", upper.astype(jnp.bfloat16), placing, preferred_element_type=jnp.float32
    ) + jnp.einsum("ibjc,ijr->brc", lower, placing, preferred_element_type=jnp.float32)
    return total.reshape(band_dev, scenes, ROWS_DEV, W)


def pack_kernel(capacity, energy_ref, spot_ref, tile_ref, count_ref, scene_ref, row_ref, out_ref):
    blocks, bands, hits = energy_ref.shape
    width = bands * hits
    slots = out_ref.shape[0]
    tiles = slots // capacity
    f32 = jnp.float32
    ii = lax.broadcasted_iota(jnp.int32, (blocks, blocks), 0)
    jj = lax.broadcasted_iota(jnp.int32, (blocks, blocks), 1)
    eye = ii == jj
    tile_row = tile_ref[...].astype(f32)
    count_row = count_ref[...].astype(f32)
    base_row = (scene_ref[...] * ROWS_DEV + row_ref[...]).astype(f32)
    zero = jnp.zeros((blocks, blocks), f32)
    count_col = jnp.sum(jnp.where(eye, count_row, zero), axis=1, keepdims=True)
    base_col = jnp.sum(jnp.where(eye, base_row, zero), axis=1, keepdims=True)
    lanes = lax.broadcasted_iota(jnp.int32, (blocks, hits), 1)
    live = lanes.astype(f32) < count_col
    spot = spot_ref[...]
    field = base_col * WIN + lax.shift_right_logical(spot, 7).astype(f32)
    column = jnp.bitwise_and(spot, W - 1).astype(f32)
    tt = lax.broadcasted_iota(jnp.int32, (tiles, blocks), 0).astype(f32)
    owners = (tt == tile_row).astype(jnp.bfloat16)
    earlier = (ii < jj).astype(jnp.bfloat16)
    before = jnp.dot(owners, earlier, preferred_element_type=f32)
    rank = jnp.sum(before * owners.astype(f32), axis=0, keepdims=True)
    place = tile_row * capacity + rank
    pp = lax.broadcasted_iota(jnp.int32, (slots, blocks), 0).astype(f32)
    select = (pp == place).astype(jnp.bfloat16)
    for band in range(bands):
        energy = energy_ref[:, band, :]
        masked = jnp.where(live, energy, jnp.zeros_like(energy))
        out_ref[:, pl.ds(band * hits, hits)] = jnp.dot(
            select, masked, preferred_element_type=f32
        ).astype(out_ref.dtype)
    out_ref[:, pl.ds(width, hits)] = jnp.dot(
        select, field.astype(jnp.bfloat16), preferred_element_type=f32
    ).astype(out_ref.dtype)
    out_ref[:, pl.ds(width + hits, hits)] = jnp.dot(
        select, column.astype(jnp.bfloat16), preferred_element_type=f32
    ).astype(out_ref.dtype)


def pack(energy, spot, tile, count, scene, row, capacity, slots):
    blocks, bands, hits = energy.shape
    width = bands * hits
    return pl.pallas_call(
        functools.partial(pack_kernel, capacity),
        out_shape=jax.ShapeDtypeStruct((slots, width + 2 * hits), energy.dtype),
    )(energy, spot, tile, count, scene, row)


def per_device(
    hit_energy,
    hit_spot,
    block_tile,
    block_count,
    block_scene,
    block_row,
    psf_bank,
    psf_index,
    response,
    conv_in,
    conv_out,
):
    tile_count = lax.axis_size("tile")
    wave_count = lax.axis_size("wave")
    block_dev, band_dev, hit_lanes = hit_energy.shape
    capacity = 2 * block_dev // tile_count
    scenes = psf_index.shape[1]
    send = pack(
        hit_energy,
        hit_spot[0],
        block_tile[0, :, 0].reshape(1, block_dev),
        block_count,
        block_scene,
        block_row,
        capacity,
        tile_count * capacity,
    )
    kern = kernel_spectra(psf_bank, psf_index, K // 2)
    got = lax.all_to_all(send, "tile", split_axis=0, concat_axis=0, tiled=True)
    got, kern = lax.optimization_barrier((got, kern))
    splat = window_splat(got, band_dev, hit_lanes, scenes)
    extended = padded_2(splat, (("tile", 2),), K // 2)
    wave_index = lax.axis_index("wave")
    my_response = lax.dynamic_slice_in_dim(response, wave_index * band_dev, band_dev, 0)
    partial = patch_blur(extended, kern, my_response, K // 2)
    color = lax.dynamic_index_in_dim(partial, wave_index, 0, keepdims=False)
    for step in range(1, wave_count):
        piece = lax.dynamic_index_in_dim(partial, (wave_index + step) % wave_count, 0, keepdims=False)
        color = color + lax.ppermute(
            piece, "wave", [(i, (i + step) % wave_count) for i in range(wave_count)]
        )
    sensor = lax.reduce_precision(color[None], exponent_bits=8, mantissa_bits=7)
    sensor = sensor.astype(jnp.bfloat16)
    rimmed = padded_2(sensor, (("tile", 2),), 2)
    hidden = jax.nn.silu(conv_rows(rimmed, conv_in))
    hidden = lax.reduce_precision(hidden, exponent_bits=8, mantissa_bits=7).astype(jnp.bfloat16)
    tile_index = lax.axis_index("tile")
    row_ids = lax.broadcasted_iota(jnp.int32, hidden.shape, 2)
    outside = ((tile_index == 0) & (row_ids == 0)) | (
        (tile_index == tile_count - 1) & (row_ids == hidden.shape[2] - 1)
    )
    hidden = jnp.where(outside, jnp.zeros_like(hidden), hidden)
    return conv_rows(hidden, conv_out).astype(jnp.bfloat16)


def solution(mesh):
    in_specs = (
        P("tile", "wave", None),
        P("wave", "tile", None),
        P("wave", "tile", None),
        P("wave", "tile"),
        P("wave", "tile"),
        P("wave", "tile"),
        P(None, "wave", None),
        P("tile", None, None),
        P(),
        P(),
        P(),
    )
    out_specs = P("wave", None, "tile", None)
    return jax.shard_map(
        per_device, mesh=mesh, in_specs=in_specs, out_specs=out_specs, check_vma=False
    )
```

```python
import functools

import jax
import jax.numpy as jnp
import numpy as np
from jax import lax
from jax.experimental import pallas as pl
from jax.sharding import PartitionSpec as P

ROWS_DEV = 16
W = 128
WIN = 4
K = 31
DFT_N = 144
LANE = 128
GROUP = 16


def padded_2(cells, sides, width):
    for axis, dim in sides:
        count = lax.axis_size(axis)
        ends = count - 1
        head = lax.slice_in_dim(cells, 0, width, axis=dim)
        tail = lax.slice_in_dim(cells, cells.shape[dim] - width, cells.shape[dim], axis=dim)
        cells = jnp.concatenate(
            [
                lax.ppermute(tail, axis, [(i, (i + 1) % count) for i in range(ends)]),
                cells,
                lax.ppermute(head, axis, [((i + 1) % count, i) for i in range(ends)]),
            ],
            axis=dim,
        )
    return cells


def conv_rows(image, weights):
    return lax.conv_general_dilated(
        image,
        weights,
        (1, 1),
        ((0, 0), (1, 1)),
        dimension_numbers=("NCHW", "OIHW", "NCHW"),
        preferred_element_type=jnp.float32,
    )


def dft_tables(width, side, radius):
    freqs = DFT_N // 2 + 1
    f = np.arange(freqs)[None, :]
    x = np.arange(width)[:, None]
    angle = 2 * np.pi * f * x / DFT_N
    forward = np.zeros((width, 2 * LANE))
    forward[:, :freqs] = np.cos(angle)
    forward[:, LANE : LANE + freqs] = -np.sin(angle)
    lag = (np.arange(side) - radius)[:, None]
    tap_angle = 2 * np.pi * f * lag / DFT_N
    taps = np.zeros((side, 2 * LANE))
    taps[:, :freqs] = np.cos(tap_angle)
    taps[:, LANE : LANE + freqs] = np.sin(tap_angle)
    weight = np.full((freqs,), 2.0)
    weight[0] = 1.0
    weight[-1] = 1.0
    back_angle = 2 * np.pi * np.arange(freqs)[:, None] * np.arange(width)[None, :] / DFT_N
    inverse = np.zeros((2 * LANE, width))
    inverse[:freqs] = weight[:, None] * np.cos(back_angle) / DFT_N
    inverse[LANE : LANE + freqs] = -weight[:, None] * np.sin(back_angle) / DFT_N
    return (
        forward.astype(np.float32),
        taps.astype(np.float32),
        inverse.astype(np.float32),
    )


def row_taps_kernel(spec_ref, kern_ref, out_ref):
    group, tall = spec_ref.shape[:2]
    rows = out_ref.shape[1]
    side = tall - rows + 1

    def one(c, carry):
        acc_re = jnp.zeros((rows, LANE), jnp.float32)
        acc_im = jnp.zeros((rows, LANE), jnp.float32)
        for u in range(side):
            xr = spec_ref[c, pl.ds(u, rows), pl.ds(0, LANE)]
            xi = spec_ref[c, pl.ds(u, rows), pl.ds(LANE, LANE)]
            kr = kern_ref[c, pl.ds(u, 1), pl.ds(0, LANE)]
            ki = kern_ref[c, pl.ds(u, 1), pl.ds(LANE, LANE)]
            acc_re = acc_re + (kr * xr - ki * xi)
            acc_im = acc_im + (kr * xi + ki * xr)
        out_ref[c, :, pl.ds(0, LANE)] = acc_re
        out_ref[c, :, pl.ds(LANE, LANE)] = acc_im
        return carry

    lax.fori_loop(0, group, one, 0)


def row_taps(spec, kern, rows):
    channels, tall, both = spec.shape
    side = kern.shape[1]
    return pl.pallas_call(
        row_taps_kernel,
        out_shape=jax.ShapeDtypeStruct((channels, rows, both), jnp.float32),
        grid=(channels // GROUP,),
        in_specs=[
            pl.BlockSpec((GROUP, tall, both), lambda g: (g, 0, 0)),
            pl.BlockSpec((GROUP, side, both), lambda g: (g, 0, 0)),
        ],
        out_specs=pl.BlockSpec((GROUP, rows, both), lambda g: (g, 0, 0)),
    )(spec, kern)


def kernel_spectra(psf_bank, psf_index, radius):
    scenes = psf_index.shape[1]
    band_dev = psf_bank.shape[1]
    side = 2 * radius + 1
    unused, taps, unused_too = dft_tables(W, side, radius)
    chosen = psf_bank[psf_index[0, :, 0]].reshape(scenes, band_dev, side, side)
    chosen = jnp.pad(chosen.transpose(1, 0, 2, 3), ((0, 0), (0, 0), (0, 1), (0, 0)))
    spectra = jnp.dot(
        chosen.reshape(-1, side), taps, precision=lax.Precision.HIGHEST
    )
    return spectra.reshape(band_dev * scenes, side + 1, -1)


def patch_blur(extended, kern, response, radius):
    band_dev, scenes, tall, width = extended.shape
    rows_dev = tall - 2 * radius
    side = 2 * radius + 1
    forward, unused, inverse = dft_tables(width, side, radius)
    hi = lax.Precision.HIGH
    spec = jnp.einsum(
        "cyx,xf->cyf", extended.reshape(band_dev * scenes, tall, width), forward, precision=hi
    )
    taps = kern
    out = row_taps(spec, taps, rows_dev).reshape(band_dev, scenes, rows_dev, -1)
    color = jnp.einsum("bsyf,bc->scyf", out, response, precision=hi)
    return jnp.einsum("scyf,fx->scyx", color, inverse, precision=hi)


def window_splat(got, band_dev, hit_lanes, scenes):
    slots = got.shape[0]
    energy = got[:, : band_dev * hit_lanes].reshape(slots, band_dev, hit_lanes)
    field = got[:, band_dev * hit_lanes : (band_dev + 1) * hit_lanes].astype(jnp.int32)
    column = got[:, (band_dev + 1) * hit_lanes :].astype(jnp.int32)
    offset = field % WIN
    base = field[:, 0] // WIN
    rows = jnp.arange(WIN, dtype=jnp.int32)
    spread = jnp.where(
        offset[:, None, None, :] == rows[None, None, :, None],
        energy[:, :, None, :],
        jnp.zeros((), energy.dtype),
    )
    onehot = (column[:, :, None] == jnp.arange(W, dtype=jnp.int32)[None, None, :]).astype(
        energy.dtype
    )
    window = jnp.einsum("ibjh,ihc->ibjc", spread, onehot, preferred_element_type=jnp.float32)
    row_ids = jnp.arange(scenes * ROWS_DEV, dtype=jnp.int32)
    placing = (base[:, None, None] + rows[None, :, None] == row_ids[None, None, :]).astype(
        jnp.float32
    )
    placing = placing.astype(jnp.bfloat16)
    upper = lax.reduce_precision(window, exponent_bits=8, mantissa_bits=7)
    lower = (window - upper).astype(jnp.bfloat16)
    total = jnp.einsum(
        "ibjc,ijr->brc", upper.astype(jnp.bfloat16), placing, preferred_element_type=jnp.float32
    ) + jnp.einsum("ibjc,ijr->brc", lower, placing, preferred_element_type=jnp.float32)
    return total.reshape(band_dev, scenes, ROWS_DEV, W)


def pack_kernel(capacity, energy_ref, spot_ref, tile_ref, count_ref, scene_ref, row_ref, out_ref):
    blocks, bands, hits = energy_ref.shape
    width = bands * hits
    slots = out_ref.shape[0]
    tiles = slots // capacity
    f32 = jnp.float32
    ii = lax.broadcasted_iota(jnp.int32, (blocks, blocks), 0)
    jj = lax.broadcasted_iota(jnp.int32, (blocks, blocks), 1)
    eye = ii == jj
    tile_row = tile_ref[...].astype(f32)
    count_row = count_ref[...].astype(f32)
    base_row = (scene_ref[...] * ROWS_DEV + row_ref[...]).astype(f32)
    zero = jnp.zeros((blocks, blocks), f32)
    count_col = jnp.sum(jnp.where(eye, count_row, zero), axis=1, keepdims=True)
    base_col = jnp.sum(jnp.where(eye, base_row, zero), axis=1, keepdims=True)
    lanes = lax.broadcasted_iota(jnp.int32, (blocks, hits), 1)
    live = lanes.astype(f32) < count_col
    spot = spot_ref[...]
    field = base_col * WIN + lax.shift_right_logical(spot, 7).astype(f32)
    column = jnp.bitwise_and(spot, W - 1).astype(f32)
    tt = lax.broadcasted_iota(jnp.int32, (tiles, blocks), 0).astype(f32)
    owners = (tt == tile_row).astype(jnp.bfloat16)
    earlier = (ii < jj).astype(jnp.bfloat16)
    before = jnp.dot(owners, earlier, preferred_element_type=f32)
    rank = jnp.sum(before * owners.astype(f32), axis=0, keepdims=True)
    place = tile_row * capacity + rank
    pp = lax.broadcasted_iota(jnp.int32, (slots, blocks), 0).astype(f32)
    select = (pp == place).astype(jnp.bfloat16)
    for band in range(bands):
        energy = energy_ref[:, band, :]
        masked = jnp.where(live, energy, jnp.zeros_like(energy))
        out_ref[:, pl.ds(band * hits, hits)] = jnp.dot(
            select, masked, preferred_element_type=f32
        ).astype(out_ref.dtype)
    out_ref[:, pl.ds(width, hits)] = jnp.dot(
        select, field.astype(jnp.bfloat16), preferred_element_type=f32
    ).astype(out_ref.dtype)
    out_ref[:, pl.ds(width + hits, hits)] = jnp.dot(
        select, column.astype(jnp.bfloat16), preferred_element_type=f32
    ).astype(out_ref.dtype)


def pack(energy, spot, tile, count, scene, row, capacity, slots):
    blocks, bands, hits = energy.shape
    width = bands * hits
    return pl.pallas_call(
        functools.partial(pack_kernel, capacity),
        out_shape=jax.ShapeDtypeStruct((slots, width + 2 * hits), energy.dtype),
    )(energy, spot, tile, count, scene, row)


def per_device(
    hit_energy,
    hit_spot,
    block_tile,
    block_count,
    block_scene,
    block_row,
    psf_bank,
    psf_index,
    response,
    conv_in,
    conv_out,
):
    tile_count = lax.axis_size("tile")
    wave_count = lax.axis_size("wave")
    block_dev, band_dev, hit_lanes = hit_energy.shape
    capacity = 2 * block_dev // tile_count
    scenes = psf_index.shape[1]
    send = pack(
        hit_energy,
        hit_spot[0],
        block_tile[0, :, 0].reshape(1, block_dev),
        block_count,
        block_scene,
        block_row,
        capacity,
        tile_count * capacity,
    )
    kern = kernel_spectra(psf_bank, psf_index, K // 2)
    got = lax.all_to_all(send, "tile", split_axis=0, concat_axis=0, tiled=True)
    got, kern = lax.optimization_barrier((got, kern))
    splat = window_splat(got, band_dev, hit_lanes, scenes)
    extended = padded_2(splat, (("tile", 2),), K // 2)
    wave_index = lax.axis_index("wave")
    my_response = lax.dynamic_slice_in_dim(response, wave_index * band_dev, band_dev, 0)
    partial = patch_blur(extended, kern, my_response, K // 2)
    color = lax.dynamic_index_in_dim(partial, wave_index, 0, keepdims=False)
    for step in range(1, wave_count):
        piece = lax.dynamic_index_in_dim(partial, (wave_index + step) % wave_count, 0, keepdims=False)
        color = color + lax.ppermute(
            piece, "wave", [(i, (i + step) % wave_count) for i in range(wave_count)]
        )
    sensor = lax.reduce_precision(color[None], exponent_bits=8, mantissa_bits=7)
    sensor = sensor.astype(jnp.bfloat16)
    rimmed = padded_2(sensor, (("tile", 2),), 2)
    hidden = jax.nn.silu(conv_rows(rimmed, conv_in))
    hidden = lax.reduce_precision(hidden, exponent_bits=8, mantissa_bits=7).astype(jnp.bfloat16)
    tile_index = lax.axis_index("tile")
    row_ids = lax.broadcasted_iota(jnp.int32, hidden.shape, 2)
    outside = ((tile_index == 0) & (row_ids == 0)) | (
        (tile_index == tile_count - 1) & (row_ids == hidden.shape[2] - 1)
    )
    hidden = jnp.where(outside, jnp.zeros_like(hidden), hidden)
    return conv_rows(hidden, conv_out).astype(jnp.bfloat16)


def solution(mesh):
    in_specs = (
        P("tile", "wave", None),
        P("wave", "tile", None),
        P("wave", "tile", None),
        P("wave", "tile"),
        P("wave", "tile"),
        P("wave", "tile"),
        P(None, "wave", None),
        P("tile", None, None),
        P(),
        P(),
        P(),
    )
    out_specs = P("wave", None, "tile", None)
    return jax.shard_map(
        per_device, mesh=mesh, in_specs=in_specs, out_specs=out_specs, check_vma=False
    )
```

```python
import functools

import jax
import jax.numpy as jnp
import numpy as np
from jax import lax
from jax.experimental import pallas as pl
from jax.sharding import PartitionSpec as P

ROWS_DEV = 16
W = 128
WIN = 4
K = 31
DFT_N = 144
LANE = 128
GROUP = 16


def padded_2(cells, sides, width):
    for axis, dim in sides:
        count = lax.axis_size(axis)
        ends = count - 1
        head = lax.slice_in_dim(cells, 0, width, axis=dim)
        tail = lax.slice_in_dim(cells, cells.shape[dim] - width, cells.shape[dim], axis=dim)
        cells = jnp.concatenate(
            [
                lax.ppermute(tail, axis, [(i, (i + 1) % count) for i in range(ends)]),
                cells,
                lax.ppermute(head, axis, [((i + 1) % count, i) for i in range(ends)]),
            ],
            axis=dim,
        )
    return cells


def conv_rows(image, weights):
    return lax.conv_general_dilated(
        image,
        weights,
        (1, 1),
        ((0, 0), (1, 1)),
        dimension_numbers=("NCHW", "OIHW", "NCHW"),
        preferred_element_type=jnp.float32,
    )


def dft_tables(width, side, radius):
    freqs = DFT_N // 2 + 1
    f = np.arange(freqs)[None, :]
    x = np.arange(width)[:, None]
    angle = 2 * np.pi * f * x / DFT_N
    forward = np.zeros((width, 2 * LANE))
    forward[:, :freqs] = np.cos(angle)
    forward[:, LANE : LANE + freqs] = -np.sin(angle)
    lag = (np.arange(side) - radius)[:, None]
    tap_angle = 2 * np.pi * f * lag / DFT_N
    taps = np.zeros((side, 2 * LANE))
    taps[:, :freqs] = np.cos(tap_angle)
    taps[:, LANE : LANE + freqs] = np.sin(tap_angle)
    weight = np.full((freqs,), 2.0)
    weight[0] = 1.0
    weight[-1] = 1.0
    back_angle = 2 * np.pi * np.arange(freqs)[:, None] * np.arange(width)[None, :] / DFT_N
    inverse = np.zeros((2 * LANE, width))
    inverse[:freqs] = weight[:, None] * np.cos(back_angle) / DFT_N
    inverse[LANE : LANE + freqs] = -weight[:, None] * np.sin(back_angle) / DFT_N
    return (
        forward.astype(np.float32),
        taps.astype(np.float32),
        inverse.astype(np.float32),
    )


def row_taps_kernel(spec_ref, kern_ref, out_ref):
    group, tall = spec_ref.shape[:2]
    rows = out_ref.shape[1]
    side = tall - rows + 1

    def one(c, carry):
        acc_re = jnp.zeros((rows, LANE), jnp.float32)
        acc_im = jnp.zeros((rows, LANE), jnp.float32)
        for u in range(side):
            xr = spec_ref[c, pl.ds(u, rows), pl.ds(0, LANE)]
            xi = spec_ref[c, pl.ds(u, rows), pl.ds(LANE, LANE)]
            kr = kern_ref[c, pl.ds(u, 1), pl.ds(0, LANE)]
            ki = kern_ref[c, pl.ds(u, 1), pl.ds(LANE, LANE)]
            acc_re = acc_re + (kr * xr - ki * xi)
            acc_im = acc_im + (kr * xi + ki * xr)
        out_ref[c, :, pl.ds(0, LANE)] = acc_re
        out_ref[c, :, pl.ds(LANE, LANE)] = acc_im
        return carry

    lax.fori_loop(0, group, one, 0)


def row_taps(spec, kern, rows):
    channels, tall, both = spec.shape
    side = kern.shape[1]
    return pl.pallas_call(
        row_taps_kernel,
        out_shape=jax.ShapeDtypeStruct((channels, rows, both), jnp.float32),
        grid=(channels // GROUP,),
        in_specs=[
            pl.BlockSpec((GROUP, tall, both), lambda g: (g, 0, 0)),
            pl.BlockSpec((GROUP, side, both), lambda g: (g, 0, 0)),
        ],
        out_specs=pl.BlockSpec((GROUP, rows, both), lambda g: (g, 0, 0)),
    )(spec, kern)


def kernel_spectra(psf_bank, psf_index, radius):
    scenes = psf_index.shape[1]
    band_dev = psf_bank.shape[1]
    side = 2 * radius + 1
    unused, taps, unused_too = dft_tables(W, side, radius)
    chosen = psf_bank[psf_index[0, :, 0]].reshape(scenes, band_dev, side, side)
    chosen = jnp.pad(chosen.transpose(1, 0, 2, 3), ((0, 0), (0, 0), (0, 1), (0, 0)))
    spectra = jnp.dot(
        chosen.reshape(-1, side), taps, precision=lax.Precision.HIGHEST
    )
    return spectra.reshape(band_dev * scenes, side + 1, -1)


def patch_blur(extended, kern, response, radius):
    band_dev, scenes, tall, width = extended.shape
    rows_dev = tall - 2 * radius
    side = 2 * radius + 1
    forward, unused, inverse = dft_tables(width, side, radius)
    hi = lax.Precision.HIGH
    spec = jnp.einsum(
        "cyx,xf->cyf", extended.reshape(band_dev * scenes, tall, width), forward, precision=hi
    )
    taps = kern
    out = row_taps(spec, taps, rows_dev).reshape(band_dev, scenes, rows_dev, -1)
    color = jnp.einsum("bsyf,bc->scyf", out, response, precision=hi)
    return jnp.einsum("scyf,fx->scyx", color, inverse, precision=hi)


def window_splat(got, band_dev, hit_lanes, scenes):
    slots = got.shape[0]
    energy = got[:, : band_dev * hit_lanes].reshape(slots, band_dev, hit_lanes)
    field = got[:, band_dev * hit_lanes : (band_dev + 1) * hit_lanes].astype(jnp.int32)
    column = got[:, (band_dev + 1) * hit_lanes :].astype(jnp.int32)
    offset = field % WIN
    base = field[:, 0] // WIN
    rows = jnp.arange(WIN, dtype=jnp.int32)
    spread = jnp.where(
        offset[:, None, None, :] == rows[None, None, :, None],
        energy[:, :, None, :],
        jnp.zeros((), energy.dtype),
    )
    onehot = (column[:, :, None] == jnp.arange(W, dtype=jnp.int32)[None, None, :]).astype(
        energy.dtype
    )
    window = jnp.einsum("ibjh,ihc->ibjc", spread, onehot, preferred_element_type=jnp.float32)
    row_ids = jnp.arange(scenes * ROWS_DEV, dtype=jnp.int32)
    placing = (base[:, None, None] + rows[None, :, None] == row_ids[None, None, :]).astype(
        jnp.float32
    )
    placing = placing.astype(jnp.bfloat16)
    upper = lax.reduce_precision(window, exponent_bits=8, mantissa_bits=7)
    lower = (window - upper).astype(jnp.bfloat16)
    parts = jnp.concatenate([upper.astype(jnp.bfloat16), lower], axis=2)
    total = jnp.einsum(
        "ibjc,ijr->brc", parts, jnp.concatenate([placing, placing], axis=1),
        preferred_element_type=jnp.float32,
    )
    return total.reshape(band_dev, scenes, ROWS_DEV, W)


def pack_kernel(capacity, energy_ref, spot_ref, tile_ref, count_ref, scene_ref, row_ref, out_ref):
    blocks, bands, hits = energy_ref.shape
    width = bands * hits
    slots = out_ref.shape[0]
    tiles = slots // capacity
    f32 = jnp.float32
    ii = lax.broadcasted_iota(jnp.int32, (blocks, blocks), 0)
    jj = lax.broadcasted_iota(jnp.int32, (blocks, blocks), 1)
    eye = ii == jj
    tile_row = tile_ref[...].astype(f32)
    count_row = count_ref[...].astype(f32)
    base_row = (scene_ref[...] * ROWS_DEV + row_ref[...]).astype(f32)
    zero = jnp.zeros((blocks, blocks), f32)
    count_col = jnp.sum(jnp.where(eye, count_row, zero), axis=1, keepdims=True)
    base_col = jnp.sum(jnp.where(eye, base_row, zero), axis=1, keepdims=True)
    lanes = lax.broadcasted_iota(jnp.int32, (blocks, hits), 1)
    live = lanes.astype(f32) < count_col
    spot = spot_ref[...]
    field = base_col * WIN + lax.shift_right_logical(spot, 7).astype(f32)
    column = jnp.bitwise_and(spot, W - 1).astype(f32)
    tt = lax.broadcasted_iota(jnp.int32, (tiles, blocks), 0).astype(f32)
    owners = (tt == tile_row).astype(jnp.bfloat16)
    earlier = (ii < jj).astype(jnp.bfloat16)
    before = jnp.dot(owners, earlier, preferred_element_type=f32)
    rank = jnp.sum(before * owners.astype(f32), axis=0, keepdims=True)
    place = tile_row * capacity + rank
    pp = lax.broadcasted_iota(jnp.int32, (slots, blocks), 0).astype(f32)
    select = (pp == place).astype(jnp.bfloat16)
    for band in range(bands):
        energy = energy_ref[:, band, :]
        masked = jnp.where(live, energy, jnp.zeros_like(energy))
        out_ref[:, pl.ds(band * hits, hits)] = jnp.dot(
            select, masked, preferred_element_type=f32
        ).astype(out_ref.dtype)
    out_ref[:, pl.ds(width, hits)] = jnp.dot(
        select, field.astype(jnp.bfloat16), preferred_element_type=f32
    ).astype(out_ref.dtype)
    out_ref[:, pl.ds(width + hits, hits)] = jnp.dot(
        select, column.astype(jnp.bfloat16), preferred_element_type=f32
    ).astype(out_ref.dtype)


def pack(energy, spot, tile, count, scene, row, capacity, slots):
    blocks, bands, hits = energy.shape
    width = bands * hits
    return pl.pallas_call(
        functools.partial(pack_kernel, capacity),
        out_shape=jax.ShapeDtypeStruct((slots, width + 2 * hits), energy.dtype),
    )(energy, spot, tile, count, scene, row)


def per_device(
    hit_energy,
    hit_spot,
    block_tile,
    block_count,
    block_scene,
    block_row,
    psf_bank,
    psf_index,
    response,
    conv_in,
    conv_out,
):
    tile_count = lax.axis_size("tile")
    wave_count = lax.axis_size("wave")
    block_dev, band_dev, hit_lanes = hit_energy.shape
    capacity = 2 * block_dev // tile_count
    scenes = psf_index.shape[1]
    send = pack(
        hit_energy,
        hit_spot[0],
        block_tile[0, :, 0].reshape(1, block_dev),
        block_count,
        block_scene,
        block_row,
        capacity,
        tile_count * capacity,
    )
    kern = kernel_spectra(psf_bank, psf_index, K // 2)
    got = lax.all_to_all(send, "tile", split_axis=0, concat_axis=0, tiled=True)
    got, kern = lax.optimization_barrier((got, kern))
    splat = window_splat(got, band_dev, hit_lanes, scenes)
    extended = padded_2(splat, (("tile", 2),), K // 2)
    wave_index = lax.axis_index("wave")
    my_response = lax.dynamic_slice_in_dim(response, wave_index * band_dev, band_dev, 0)
    partial = patch_blur(extended, kern, my_response, K // 2)
    color = lax.dynamic_index_in_dim(partial, wave_index, 0, keepdims=False)
    for step in range(1, wave_count):
        piece = lax.dynamic_index_in_dim(partial, (wave_index + step) % wave_count, 0, keepdims=False)
        color = color + lax.ppermute(
            piece, "wave", [(i, (i + step) % wave_count) for i in range(wave_count)]
        )
    sensor = lax.reduce_precision(color[None], exponent_bits=8, mantissa_bits=7)
    sensor = sensor.astype(jnp.bfloat16)
    rimmed = padded_2(sensor, (("tile", 2),), 2)
    hidden = jax.nn.silu(conv_rows(rimmed, conv_in))
    hidden = lax.reduce_precision(hidden, exponent_bits=8, mantissa_bits=7).astype(jnp.bfloat16)
    tile_index = lax.axis_index("tile")
    row_ids = lax.broadcasted_iota(jnp.int32, hidden.shape, 2)
    outside = ((tile_index == 0) & (row_ids == 0)) | (
        (tile_index == tile_count - 1) & (row_ids == hidden.shape[2] - 1)
    )
    hidden = jnp.where(outside, jnp.zeros_like(hidden), hidden)
    return conv_rows(hidden, conv_out).astype(jnp.bfloat16)


def solution(mesh):
    in_specs = (
        P("tile", "wave", None),
        P("wave", "tile", None),
        P("wave", "tile", None),
        P("wave", "tile"),
        P("wave", "tile"),
        P("wave", "tile"),
        P(None, "wave", None),
        P("tile", None, None),
        P(),
        P(),
        P(),
    )
    out_specs = P("wave", None, "tile", None)
    return jax.shard_map(
        per_device, mesh=mesh, in_specs=in_specs, out_specs=out_specs, check_vma=False
    )
```

```python
import functools

import jax
import jax.numpy as jnp
import numpy as np
from jax import lax
from jax.experimental import pallas as pl
from jax.sharding import PartitionSpec as P

ROWS_DEV = 16
W = 128
WIN = 4
K = 31
DFT_N = 144
LANE = 128
GROUP = 16


def padded_2(cells, sides, width):
    for axis, dim in sides:
        count = lax.axis_size(axis)
        ends = count - 1
        head = lax.slice_in_dim(cells, 0, width, axis=dim)
        tail = lax.slice_in_dim(cells, cells.shape[dim] - width, cells.shape[dim], axis=dim)
        cells = jnp.concatenate(
            [
                lax.ppermute(tail, axis, [(i, (i + 1) % count) for i in range(ends)]),
                cells,
                lax.ppermute(head, axis, [((i + 1) % count, i) for i in range(ends)]),
            ],
            axis=dim,
        )
    return cells


def conv_rows(image, weights):
    return lax.conv_general_dilated(
        image,
        weights,
        (1, 1),
        ((0, 0), (1, 1)),
        dimension_numbers=("NCHW", "OIHW", "NCHW"),
        preferred_element_type=jnp.float32,
    )


def dft_tables(width, side, radius):
    freqs = DFT_N // 2 + 1
    f = np.arange(freqs)[None, :]
    x = np.arange(width)[:, None]
    angle = 2 * np.pi * f * x / DFT_N
    forward = np.zeros((width, 2 * LANE))
    forward[:, :freqs] = np.cos(angle)
    forward[:, LANE : LANE + freqs] = -np.sin(angle)
    lag = (np.arange(side) - radius)[:, None]
    tap_angle = 2 * np.pi * f * lag / DFT_N
    taps = np.zeros((side, 2 * LANE))
    taps[:, :freqs] = np.cos(tap_angle)
    taps[:, LANE : LANE + freqs] = np.sin(tap_angle)
    weight = np.full((freqs,), 2.0)
    weight[0] = 1.0
    weight[-1] = 1.0
    back_angle = 2 * np.pi * np.arange(freqs)[:, None] * np.arange(width)[None, :] / DFT_N
    inverse = np.zeros((2 * LANE, width))
    inverse[:freqs] = weight[:, None] * np.cos(back_angle) / DFT_N
    inverse[LANE : LANE + freqs] = -weight[:, None] * np.sin(back_angle) / DFT_N
    return (
        forward.astype(np.float32),
        taps.astype(np.float32),
        inverse.astype(np.float32),
    )


def row_taps_kernel(spec_ref, kern_ref, out_ref):
    group, tall = spec_ref.shape[:2]
    rows = out_ref.shape[1]
    side = tall - rows + 1

    def one(c, carry):
        acc_re = jnp.zeros((rows, LANE), jnp.float32)
        acc_im = jnp.zeros((rows, LANE), jnp.float32)
        for u in range(side):
            xr = spec_ref[c, pl.ds(u, rows), pl.ds(0, LANE)]
            xi = spec_ref[c, pl.ds(u, rows), pl.ds(LANE, LANE)]
            kr = kern_ref[c, pl.ds(u, 1), pl.ds(0, LANE)]
            ki = kern_ref[c, pl.ds(u, 1), pl.ds(LANE, LANE)]
            acc_re = acc_re + (kr * xr - ki * xi)
            acc_im = acc_im + (kr * xi + ki * xr)
        out_ref[c, :, pl.ds(0, LANE)] = acc_re
        out_ref[c, :, pl.ds(LANE, LANE)] = acc_im
        return carry

    lax.fori_loop(0, group, one, 0)


def row_taps(spec, kern, rows):
    channels, tall, both = spec.shape
    side = kern.shape[1]
    return pl.pallas_call(
        row_taps_kernel,
        out_shape=jax.ShapeDtypeStruct((channels, rows, both), jnp.float32),
        grid=(channels // GROUP,),
        in_specs=[
            pl.BlockSpec((GROUP, tall, both), lambda g: (g, 0, 0)),
            pl.BlockSpec((GROUP, side, both), lambda g: (g, 0, 0)),
        ],
        out_specs=pl.BlockSpec((GROUP, rows, both), lambda g: (g, 0, 0)),
    )(spec, kern)


def kernel_spectra(psf_bank, psf_index, radius):
    scenes = psf_index.shape[1]
    band_dev = psf_bank.shape[1]
    side = 2 * radius + 1
    unused, taps, unused_too = dft_tables(W, side, radius)
    chosen = psf_bank[psf_index[0, :, 0]].reshape(scenes, band_dev, side, side)
    chosen = jnp.pad(chosen.transpose(1, 0, 2, 3), ((0, 0), (0, 0), (0, 1), (0, 0)))
    spectra = jnp.dot(
        chosen.reshape(-1, side), taps, precision=lax.Precision.HIGHEST
    )
    return spectra.reshape(band_dev * scenes, side + 1, -1)


def patch_blur(extended, kern, response, radius):
    band_dev, scenes, tall, width = extended.shape
    rows_dev = tall - 2 * radius
    side = 2 * radius + 1
    forward, unused, inverse = dft_tables(width, side, radius)
    hi = lax.Precision.HIGH
    spec = jnp.einsum(
        "cyx,xf->cyf", extended.reshape(band_dev * scenes, tall, width), forward, precision=hi
    )
    taps = kern
    out = row_taps(spec, taps, rows_dev).reshape(band_dev, scenes, rows_dev, -1)
    color = jnp.einsum("bsyf,bc->scyf", out, response, precision=hi)
    return jnp.einsum("scyf,fx->scyx", color, inverse, precision=hi)


def window_splat(got, band_dev, hit_lanes, scenes):
    slots = got.shape[0]
    energy = got[:, : band_dev * hit_lanes].reshape(slots, band_dev, hit_lanes)
    field = got[:, band_dev * hit_lanes : (band_dev + 1) * hit_lanes].astype(jnp.int32)
    column = got[:, (band_dev + 1) * hit_lanes :].astype(jnp.int32)
    offset = field % WIN
    base = field[:, 0] // WIN
    rows = jnp.arange(WIN, dtype=jnp.int32)
    spread = jnp.where(
        offset[:, None, None, :] == rows[None, None, :, None],
        energy[:, :, None, :],
        jnp.zeros((), energy.dtype),
    )
    onehot = (column[:, :, None] == jnp.arange(W, dtype=jnp.int32)[None, None, :]).astype(
        energy.dtype
    )
    window = jnp.einsum("ibjh,ihc->ibjc", spread, onehot, preferred_element_type=jnp.float32)
    row_ids = jnp.arange(scenes * ROWS_DEV, dtype=jnp.int32)
    placing = (base[:, None, None] + rows[None, :, None] == row_ids[None, None, :]).astype(
        jnp.float32
    )
    placing = placing.astype(jnp.bfloat16)
    upper = lax.reduce_precision(window, exponent_bits=8, mantissa_bits=7)
    lower = (window - upper).astype(jnp.bfloat16)
    total = jnp.einsum(
        "ibjc,ijr->brc", upper.astype(jnp.bfloat16), placing, preferred_element_type=jnp.float32
    ) + jnp.einsum("ibjc,ijr->brc", lower, placing, preferred_element_type=jnp.float32)
    return total.reshape(band_dev, scenes, ROWS_DEV, W)


def pack_kernel(capacity, energy_ref, spot_ref, tile_ref, count_ref, scene_ref, row_ref, out_ref):
    blocks, bands, hits = energy_ref.shape
    width = bands * hits
    slots = out_ref.shape[0]
    tiles = slots // capacity
    f32 = jnp.float32
    ii = lax.broadcasted_iota(jnp.int32, (blocks, blocks), 0)
    jj = lax.broadcasted_iota(jnp.int32, (blocks, blocks), 1)
    eye = ii == jj
    tile_row = tile_ref[...].astype(f32)
    count_row = count_ref[...].astype(f32)
    base_row = (scene_ref[...] * ROWS_DEV + row_ref[...]).astype(f32)
    zero = jnp.zeros((blocks, blocks), f32)
    count_col = jnp.sum(jnp.where(eye, count_row, zero), axis=1, keepdims=True)
    base_col = jnp.sum(jnp.where(eye, base_row, zero), axis=1, keepdims=True)
    lanes = lax.broadcasted_iota(jnp.int32, (blocks, hits), 1)
    live = lanes.astype(f32) < count_col
    spot = spot_ref[...]
    field = base_col * WIN + lax.shift_right_logical(spot, 7).astype(f32)
    column = jnp.bitwise_and(spot, W - 1).astype(f32)
    tt = lax.broadcasted_iota(jnp.int32, (tiles, blocks), 0).astype(f32)
    owners = (tt == tile_row).astype(jnp.bfloat16)
    earlier = (ii < jj).astype(jnp.bfloat16)
    before = jnp.dot(owners, earlier, preferred_element_type=f32)
    rank = jnp.sum(before * owners.astype(f32), axis=0, keepdims=True)
    place = tile_row * capacity + rank
    pp = lax.broadcasted_iota(jnp.int32, (slots, blocks), 0).astype(f32)
    select = (pp == place).astype(jnp.bfloat16)
    for band in range(bands):
        energy = energy_ref[:, band, :]
        masked = jnp.where(live, energy, jnp.zeros_like(energy))
        out_ref[:, pl.ds(band * hits, hits)] = jnp.dot(
            select, masked, preferred_element_type=f32
        ).astype(out_ref.dtype)
    out_ref[:, pl.ds(width, hits)] = jnp.dot(
        select, field.astype(jnp.bfloat16), preferred_element_type=f32
    ).astype(out_ref.dtype)
    out_ref[:, pl.ds(width + hits, hits)] = jnp.dot(
        select, column.astype(jnp.bfloat16), preferred_element_type=f32
    ).astype(out_ref.dtype)


def pack(energy, spot, tile, count, scene, row, capacity, slots):
    blocks, bands, hits = energy.shape
    width = bands * hits
    return pl.pallas_call(
        functools.partial(pack_kernel, capacity),
        out_shape=jax.ShapeDtypeStruct((slots, width + 2 * hits), energy.dtype),
    )(energy, spot, tile, count, scene, row)


def per_device(
    hit_energy,
    hit_spot,
    block_tile,
    block_count,
    block_scene,
    block_row,
    psf_bank,
    psf_index,
    response,
    conv_in,
    conv_out,
):
    tile_count = lax.axis_size("tile")
    wave_count = lax.axis_size("wave")
    block_dev, band_dev, hit_lanes = hit_energy.shape
    capacity = 2 * block_dev // tile_count
    scenes = psf_index.shape[1]
    send = pack(
        hit_energy,
        hit_spot[0],
        block_tile[0, :, 0].reshape(1, block_dev),
        block_count,
        block_scene,
        block_row,
        capacity,
        tile_count * capacity,
    )
    kern = kernel_spectra(psf_bank, psf_index, K // 2)
    got = lax.all_to_all(send, "tile", split_axis=0, concat_axis=0, tiled=True)
    got, kern = lax.optimization_barrier((got, kern))
    splat = window_splat(got, band_dev, hit_lanes, scenes)
    count = tile_count
    radius = K // 2
    above = lax.ppermute(splat, "tile", [(i, i + 1) for i in range(count - 1)])
    below = lax.ppermute(splat, "tile", [(i + 1, i) for i in range(count - 1)])
    extended = jnp.concatenate(
        [above[:, :, ROWS_DEV - radius :], splat, below[:, :, :radius]], axis=2
    )
    wave_index = lax.axis_index("wave")
    my_response = lax.dynamic_slice_in_dim(response, wave_index * band_dev, band_dev, 0)
    partial = patch_blur(extended, kern, my_response, K // 2)
    color = lax.dynamic_index_in_dim(partial, wave_index, 0, keepdims=False)
    for step in range(1, wave_count):
        piece = lax.dynamic_index_in_dim(partial, (wave_index + step) % wave_count, 0, keepdims=False)
        color = color + lax.ppermute(
            piece, "wave", [(i, (i + step) % wave_count) for i in range(wave_count)]
        )
    sensor = lax.reduce_precision(color[None], exponent_bits=8, mantissa_bits=7)
    sensor = sensor.astype(jnp.bfloat16)
    rimmed = padded_2(sensor, (("tile", 2),), 2)
    hidden = jax.nn.silu(conv_rows(rimmed, conv_in))
    hidden = lax.reduce_precision(hidden, exponent_bits=8, mantissa_bits=7).astype(jnp.bfloat16)
    tile_index = lax.axis_index("tile")
    row_ids = lax.broadcasted_iota(jnp.int32, hidden.shape, 2)
    outside = ((tile_index == 0) & (row_ids == 0)) | (
        (tile_index == tile_count - 1) & (row_ids == hidden.shape[2] - 1)
    )
    hidden = jnp.where(outside, jnp.zeros_like(hidden), hidden)
    return conv_rows(hidden, conv_out).astype(jnp.bfloat16)


def solution(mesh):
    in_specs = (
        P("tile", "wave", None),
        P("wave", "tile", None),
        P("wave", "tile", None),
        P("wave", "tile"),
        P("wave", "tile"),
        P("wave", "tile"),
        P(None, "wave", None),
        P("tile", None, None),
        P(),
        P(),
        P(),
    )
    out_specs = P("wave", None, "tile", None)
    return jax.shard_map(
        per_device, mesh=mesh, in_specs=in_specs, out_specs=out_specs, check_vma=False
    )
```
